128 devices in a mesh: dom: 32 (over y, x, core), ref: 4 (over z).
Axes of the slice: x: 4, y: 4, z: 4, core: 2. Of those that a mesh axis runs over, the one named last changes fastest.
Arguments:
- particles: bfloat16 [32768, 16384], P(('dom', 'ref')), may hold values from -12 to 12
- noise_prec: bfloat16 [32768], P(('dom', 'ref')), may hold values from 0.25 to 2
- prior_pose: int32 [32768], P(('dom', 'ref')), may hold values from 0 to 4607
- owners: int32 [32768], P(('dom', 'ref')), may hold values from 0 to 31, as said below
- projections: bfloat16 [32, 64, 16384], P('ref', 'dom'), may hold values from -4 to 4
- pose_index: int32 [64], P('dom'), may hold values from 0 to 4607
Outputs:
- class_prob: float32 [32768, 32], P(('dom', 'ref'))
- log_like: float32 [32768], P(('dom', 'ref'))
- class_sums: bfloat16 [32, 64, 16384], P('ref', 'dom')
- weight_totals: float32 [32, 64], P('ref', 'dom')
The draws below stay inside these ranges and needn't reach their ends.
Inputs may be any that keep to these rules, and one draw needn't show every extreme that they name: `owners`: the particles of one device name each owner at most 10 times; in every ref row some owner is named exactly 10 times by every device of that row.
All inputs are finite; a program needn't handle non-finite values.
Results may differ from the reference program's by a relative error of at most 0.015.
Values may be sent and summed in bfloat16 or wider, within the bound.
No kernel may reach another device: no remote copies, remote signals or barrier semaphores. Data moves between devices by JAX's collectives and lax.ppermute only.
A program may use at most 128 MiB of HBM per device.

```python
import math
import jax
import jax.numpy as jnp
from jax import lax

IMG = 128
PIX = 16384
CLS = 32
PD = 2
POSES = 64
B_DEV = 256
SHIFTS = 3
GRID = 4608
PRIOR_WIDTH = 576
CAP = 10
SLOTS = 320
PARTS_SIZE = 32768
N_DOM = 32
N_REF = 4


def owner_table(key):
    device_count = N_DOM * N_REF
    hot_owner = jax.random.randint(jax.random.fold_in(key, 11), (N_REF,), 0, N_DOM)
    device_keys = jax.random.split(jax.random.fold_in(key, 12), device_count)
    other_slots = (N_DOM - 1) * CAP

    def one_device(device_key, hot_one):
        first_key, second_key = jax.random.split(device_key)
        chosen = jax.random.permutation(first_key, other_slots)[:B_DEV - CAP]
        others = (chosen // CAP).astype(jnp.int32)
        others = others + (others >= hot_one).astype(jnp.int32)
        listed = jnp.concatenate([jnp.full((CAP,), hot_one, jnp.int32), others])
        return jax.random.permutation(second_key, listed)
    hot_each = jnp.tile(hot_owner, N_DOM)
    return jax.vmap(one_device)(device_keys, hot_each).reshape(-1).astype(jnp.int32)


def projection_row(key, row_id):
    row_key = jax.random.fold_in(jax.random.fold_in(key, 21), row_id)
    values = jax.random.normal(row_key, (PIX,), jnp.float32)
    return jnp.clip(values, -4.0, 4.0)


def draw_owners(key, part):
    return owner_table(key)


def draw_projections(key, part):
    row_ids = jnp.arange(CLS * POSES, dtype=jnp.int32)

    def one_row(row_id):
        return projection_row(key, row_id)
    return lax.map(one_row, row_ids).reshape(CLS, POSES, PIX).astype(jnp.bfloat16)


def draw_particles(key, part):
    owner_ids = owner_table(key)
    pick_keys = jax.random.split(jax.random.fold_in(key, 31), 4)
    classes = jax.random.randint(pick_keys[0], (PARTS_SIZE,), 0, CLS)
    local_pose = jax.random.randint(pick_keys[1], (PARTS_SIZE,), 0, PD)
    offsets = jax.random.randint(pick_keys[2], (PARTS_SIZE,), 0, SHIFTS) - SHIFTS // 2
    poses = owner_ids * PD + local_pose
    amplitude = jnp.exp(jax.random.uniform(pick_keys[3], (PARTS_SIZE,), jnp.float32, jnp.log(1.5), jnp.log(6.0)))
    second_weight = jnp.zeros((PARTS_SIZE,), jnp.float32)
    other_class = classes
    noise_key = jax.random.fold_in(key, 41)

    def one_particle(inputs):
        class_one, other_one, pose_one, offset_one, amp_one, second_one, index_one = inputs
        main_row = projection_row(key, class_one * POSES + pose_one)
        extra_row = projection_row(key, other_one * POSES + pose_one)
        image = (main_row + second_one * extra_row) * (amp_one * 1.28 / IMG)
        image = jnp.roll(image.reshape(IMG, IMG), -offset_one, axis=1).reshape(PIX)
        noise = jnp.clip(jax.random.normal(jax.random.fold_in(noise_key, index_one), (PIX,), jnp.float32), -4.5, 4.5)
        return image + noise
    indices = jnp.arange(PARTS_SIZE, dtype=jnp.int32)
    return lax.map(one_particle, (classes, other_class, poses, offsets, amplitude, second_weight, indices)).astype(jnp.bfloat16)


def place_ends(entries, key, smallest, largest):
    spot = [jax.random.randint(jax.random.fold_in(key, axis), (), 0, length) for axis, length in enumerate(entries.shape)]
    main_axis = entries.shape.index(max(entries.shape))
    next_to = spot[:main_axis] + [(spot[main_axis] + 1) % entries.shape[main_axis]] + spot[main_axis + 1:]
    return entries.at[tuple(spot)].set(smallest).at[tuple(next_to)].set(largest)


def block_levels(key, extent, shards, least, largest):
    level, own = 1.0, jax.random.fold_in(key, 6)
    for position, blocks in shards:
        heights = jnp.exp(jax.random.uniform(jax.random.fold_in(own, position), (blocks,), jnp.float32, least / len(shards), largest / len(shards)))
        level = level * jnp.repeat(heights, extent[position] // blocks).reshape([-1 if axis == position else 1 for axis in range(len(extent))])
    return level


def setup_inputs(seed: int = 0) -> dict:
    arg_keys = jax.random.split(jax.random.key(seed), 7)
    return {
        "particles": draw_particles(jax.random.fold_in(arg_keys[6], 71), 0),
        "noise_prec": jnp.clip(jnp.exp(math.log(2.0) - 2.0794415 * jax.random.uniform(arg_keys[1], (PARTS_SIZE,), jnp.float32) ** block_levels(arg_keys[1], (PARTS_SIZE,), ((0, 128),), -0.2, 0.2)), 0.25, 2.0).astype(jnp.bfloat16),
        "prior_pose": place_ends(jax.random.randint(arg_keys[2], (PARTS_SIZE,), 0, GRID), jax.random.fold_in(arg_keys[2], 1), 0, GRID - 1).astype(jnp.int32),
        "owners": draw_owners(jax.random.fold_in(arg_keys[6], 71), 0),
        "projections": draw_projections(jax.random.fold_in(arg_keys[6], 71), 0),
        "pose_index": place_ends(jax.random.randint(arg_keys[5], (POSES,), 0, GRID), jax.random.fold_in(arg_keys[5], 1), 0, GRID - 1).astype(jnp.int32),
    }


def translate(images, offset):
    full_shape = images.shape
    squares = images.reshape(full_shape[:-1] + (IMG, IMG))
    return jnp.roll(squares, offset, axis=-1).reshape(full_shape)


def reference(particles, noise_prec, prior_pose, owners, projections, pose_index):
    device = jnp.arange(PARTS_SIZE, dtype=jnp.int32) // B_DEV
    dom_of = device // N_REF
    ref_of = device % N_REF
    grouped = owners.reshape(N_DOM * N_REF, B_DEV)
    earlier = jnp.arange(B_DEV)[:, None] > jnp.arange(B_DEV)[None, :]
    same_owner = grouped[:, :, None] == grouped[:, None, :]
    slot_rank = jnp.sum(same_owner & earlier[None], axis=2).astype(jnp.int32).reshape(PARTS_SIZE)
    slot_of = dom_of * CAP + slot_rank
    flat_index = (ref_of * N_DOM + owners) * SLOTS + slot_of
    slot_table = jnp.full((N_REF * N_DOM * SLOTS,), PARTS_SIZE, jnp.int32)
    slot_table = slot_table.at[flat_index].set(jnp.arange(PARTS_SIZE, dtype=jnp.int32)).reshape(N_REF, N_DOM, SLOTS)
    padded_img = jnp.concatenate([particles, jnp.zeros((1, PIX), particles.dtype)], axis=0)
    padded_prec = jnp.concatenate([noise_prec.astype(jnp.float32), jnp.zeros((1,), jnp.float32)])
    padded_prior = jnp.concatenate([prior_pose, jnp.full((1,), -1, jnp.int32)])
    norms = jnp.sum(jnp.square(projections.astype(jnp.float32)), axis=2)
    offsets = [u - SHIFTS // 2 for u in range(SHIFTS)]

    def per_owner(g):
        members = slot_table[:, g, :]
        images = padded_img[members]
        precision = padded_prec[members]
        prior_ids = padded_prior[members]
        live_slot = (prior_ids >= 0).astype(jnp.float32)
        group_proj = lax.dynamic_slice_in_dim(projections, g * PD, PD, 1).astype(jnp.float32)
        group_norm = lax.dynamic_slice_in_dim(norms, g * PD, PD, 1)
        group_index = lax.dynamic_slice_in_dim(pose_index, g * PD, PD, 0)
        stacked = jnp.stack([translate(images, t) for t in offsets]).astype(jnp.float32)
        correlation = jnp.einsum('arsp,cjp->arscj', stacked, group_proj)
        log_prior = -jnp.abs(group_index[None, None, :] - prior_ids[:, :, None]).astype(jnp.float32) / PRIOR_WIDTH
        scores = precision[None, :, :, None, None] * (correlation / IMG - group_norm[None, None, None] / (2.0 * IMG * IMG))
        scores = scores + log_prior[None, :, :, None, :]
        highest = jnp.max(scores, axis=(0, 3, 4))
        loglike = highest + jnp.log(jnp.sum(jnp.exp(scores - highest[None, :, :, None, None]), axis=(0, 3, 4)))
        weights = jnp.exp(scores - loglike[None, :, :, None, None]) * live_slot[None, :, :, None, None]
        class_post = jnp.sum(weights, axis=(0, 4))
        low_weights = weights.astype(jnp.bfloat16)
        partial_value = jnp.einsum('arscj,arsp->rcjp', low_weights.astype(jnp.float32), stacked).astype(jnp.bfloat16)
        owner_sums = jnp.sum(partial_value.astype(jnp.float32), axis=0).astype(jnp.bfloat16)
        totals = jnp.sum(weights, axis=(0, 1, 2))
        return owner_sums, totals, class_post, loglike

    owner_sums, owner_totals, owner_prob, owner_like = lax.map(per_owner, jnp.arange(N_DOM, dtype=jnp.int32))
    class_sums = jnp.transpose(owner_sums, (1, 0, 2, 3)).reshape(CLS, POSES, PIX)
    weight_totals = jnp.transpose(owner_totals, (1, 0, 2)).reshape(CLS, POSES)
    class_prob = owner_prob[owners, ref_of, slot_of]
    log_like = owner_like[owners, ref_of, slot_of]
    return class_prob, log_like, class_sums, weight_totals
```

```python
import jax
import jax.numpy as jnp
from jax import lax
from jax.sharding import PartitionSpec as P

IMG = 128
SHIFTS = 3
PRIOR_WIDTH = 576
FIRST_ROWS = 8


def translate(images, offset):
    if offset == 0:
        return images
    pixels = images.shape[-1]
    lane = lax.broadcasted_iota(jnp.int32, images.shape, images.ndim - 1) % IMG
    near = jnp.roll(images, offset, axis=-1)
    if offset > 0:
        far = jnp.roll(images, offset - IMG, axis=-1)
        keep = lane >= offset
    else:
        far = jnp.roll(images, offset + IMG, axis=-1)
        keep = lane < IMG + offset
    del pixels
    return jnp.where(keep, near, far)


def shards(particles, noise_prec, prior_pose, owners, projections, pose_index):
    f32 = jnp.float32
    count_dom = lax.axis_size("dom")
    count_ref = lax.axis_size("ref")
    arrived, pixels = particles.shape
    capacity = (5 * arrived + 4 * count_dom - 1) // (4 * count_dom)
    rows_a = min(FIRST_ROWS, capacity)
    rows_b = capacity - rows_a

    earlier = jnp.arange(arrived)[:, None] > jnp.arange(arrived)[None, :]
    same_owner = owners[:, None] == owners[None, :]
    slot_rank = jnp.sum(same_owner & earlier, axis=1).astype(jnp.int32)
    in_a = slot_rank < rows_a

    def pick(slot_of, count):
        return slot_of[None, :] == jnp.arange(count, dtype=jnp.int32)[:, None]

    pick_a = pick(jnp.where(in_a, owners * rows_a + slot_rank, -1), count_dom * rows_a)
    send_a = jnp.dot(pick_a.astype(particles.dtype), particles, preferred_element_type=f32)
    send_a = send_a.astype(particles.dtype).reshape(count_dom, rows_a, pixels)
    pick_all = pick(owners * capacity + slot_rank, count_dom * capacity)
    send_prec = jnp.sum(jnp.where(pick_all, noise_prec.astype(f32)[None, :], 0.0), axis=1)
    send_prior = jnp.sum(jnp.where(pick_all, prior_pose.astype(f32)[None, :] + 1.0, 0.0), axis=1) - 1.0
    meta = jnp.stack(
        [send_prec.reshape(count_dom, capacity), send_prior.reshape(count_dom, capacity)], axis=1
    )
    got_meta = lax.all_to_all(meta, "dom", 0, 0, tiled=True)
    got_a = lax.all_to_all(send_a, "dom", 0, 0, tiled=True).reshape(count_dom * rows_a, pixels)
    if rows_b:
        pick_b = pick(jnp.where(in_a, -1, owners * rows_b + slot_rank - rows_a), count_dom * rows_b)
        send_b = jnp.dot(pick_b.astype(particles.dtype), particles, preferred_element_type=f32)
        send_b = send_b.astype(particles.dtype).reshape(count_dom, rows_b, pixels)
        got_a, send_b = lax.optimization_barrier((got_a, send_b))
        got_b = lax.all_to_all(send_b, "dom", 0, 0, tiled=True).reshape(count_dom * rows_b, pixels)

    own_proj = projections.reshape(-1, pixels)
    all_proj = lax.all_gather(own_proj, "ref", axis=0, tiled=True)
    rows = all_proj.shape[0]
    offsets = [u - SHIFTS // 2 for u in range(SHIFTS)]
    shifted = jnp.concatenate([translate(all_proj, -t) for t in offsets], axis=0)
    norms = jnp.sum(jnp.square(all_proj.astype(f32)), axis=1)
    per_class = projections.shape[1]
    pose_f = pose_index.astype(f32)

    def part(images, precision, prior_ids):
        n = images.shape[0]
        live = (prior_ids >= 0).astype(f32)
        corr = lax.dot_general(
            images, shifted, (((1,), (1,)), ((), ())), preferred_element_type=f32
        ).reshape(n, SHIFTS, rows)
        log_prior = -jnp.abs(pose_f[None, :] - prior_ids[:, None]) / PRIOR_WIDTH
        prior_rows = jnp.tile(log_prior, (1, rows // per_class))
        scaled = corr / IMG - norms[None, None, :] / (2.0 * IMG * IMG)
        scores = precision[:, None, None] * scaled + prior_rows[:, None, :]
        highest = jnp.max(scores, axis=(1, 2))
        loglike = highest + jnp.log(jnp.sum(jnp.exp(scores - highest[:, None, None]), axis=(1, 2)))
        weights = jnp.exp(scores - loglike[:, None, None]) * live[:, None, None]
        class_post = jnp.sum(weights.reshape(n, SHIFTS, rows // per_class, per_class), axis=(1, 3))
        totals = jnp.sum(weights, axis=(0, 1))
        low = weights.astype(jnp.bfloat16).reshape(n, SHIFTS * rows)
        summed = lax.dot_general(low, images, (((0,), (0,)), ((), ())), preferred_element_type=f32)
        post = jnp.concatenate([class_post, loglike[:, None]], axis=1)
        return summed, totals, post

    meta_prec = got_meta[:, 0, :]
    meta_prior = got_meta[:, 1, :]
    sum_a, tot_a, post_a = part(
        got_a, meta_prec[:, :rows_a].reshape(-1), meta_prior[:, :rows_a].reshape(-1)
    )
    post_width = post_a.shape[1]
    back = [post_a.reshape(count_dom, rows_a, post_width)]
    if rows_b:
        sum_b, tot_b, post_b = part(
            got_b, meta_prec[:, rows_a:].reshape(-1), meta_prior[:, rows_a:].reshape(-1)
        )
        sum_a = sum_a + sum_b
        tot_a = tot_a + tot_b
        back.append(post_b.reshape(count_dom, rows_b, post_width))
    back = jnp.concatenate(back, axis=1)
    got_back = lax.all_to_all(back, "dom", 0, 0, tiled=True).reshape(count_dom * capacity, post_width)

    per_shift = sum_a.reshape(SHIFTS, rows, pixels)
    image_sums = translate(per_shift[0], offsets[0])
    for u in range(1, SHIFTS):
        image_sums = image_sums + translate(per_shift[u], offsets[u])
    partial = image_sums.astype(jnp.bfloat16).reshape(count_ref, rows // count_ref, pixels)
    got_partial = lax.all_to_all(partial, "ref", 0, 0, tiled=True)
    class_sums = jnp.sum(got_partial.astype(f32), axis=0).astype(jnp.bfloat16)
    class_sums = class_sums.reshape(projections.shape)
    got_tot = lax.all_to_all(tot_a.reshape(count_ref, rows // count_ref), "ref", 0, 0, tiled=True)
    weight_totals = jnp.sum(got_tot, axis=0).reshape(projections.shape[0], projections.shape[1])

    mine = got_back[owners * capacity + slot_rank]
    class_prob = mine[:, : post_width - 1]
    log_like = mine[:, post_width - 1]
    return (class_prob, log_like, class_sums, weight_totals)


def solution(mesh):
    in_specs = (
        P(("dom", "ref"), None),
        P(("dom", "ref")),
        P(("dom", "ref")),
        P(("dom", "ref")),
        P("ref", "dom", None),
        P("dom"),
    )
    out_specs = (P(("dom", "ref"), None), P(("dom", "ref")), P("ref", "dom", None), P("ref", "dom"))
    return jax.shard_map(shards, mesh=mesh, in_specs=in_specs, out_specs=out_specs, check_vma=False)
```

```python
import functools

import jax
import jax.numpy as jnp
from jax import lax
from jax.experimental import pallas as pl
from jax.experimental.pallas import tpu as pltpu
from jax.sharding import PartitionSpec as P

IMG = 128
SHIFTS = 3
PRIOR_WIDTH = 576
FIRST_ROWS = 8
CHUNK = 2048


def translate(images, offset):
    if offset == 0:
        return images
    pixels = images.shape[-1]
    lane = lax.broadcasted_iota(jnp.int32, images.shape, images.ndim - 1) % IMG
    near = jnp.roll(images, offset, axis=-1)
    if offset > 0:
        far = jnp.roll(images, offset - IMG, axis=-1)
        keep = lane >= offset
    else:
        far = jnp.roll(images, offset + IMG, axis=-1)
        keep = lane < IMG + offset
    del pixels
    return jnp.where(keep, near, far)


def sums_kernel(offsets, rows, wa_ref, xa_ref, wb_ref, xb_ref, out_ref):
    y = jnp.dot(wa_ref[...], xa_ref[...], preferred_element_type=jnp.float32)
    y = y + jnp.dot(wb_ref[...], xb_ref[...], preferred_element_type=jnp.float32)
    for j in range(out_ref.shape[1] // IMG):
        acc = None
        for u, t in enumerate(offsets):
            blk = y[u * rows:(u + 1) * rows, j * IMG:(j + 1) * IMG]
            if t % IMG:
                blk = pltpu.roll(blk, shift=t % IMG, axis=1)
            acc = blk if acc is None else acc + blk
        out_ref[:, j * IMG:(j + 1) * IMG] = acc.astype(out_ref.dtype)


def class_image_sums(wa, xa, wb, xb, offsets):
    rows = wa.shape[0] // len(offsets)
    pixels = xa.shape[1]
    chunk = min(CHUNK, pixels)
    flops = 2 * wa.shape[0] * pixels * (xa.shape[0] + xb.shape[0])
    bytes_accessed = 2 * (xa.size + xb.size + wa.size + wb.size + rows * pixels)
    return pl.pallas_call(
        functools.partial(sums_kernel, tuple(offsets), rows),
        grid=(pixels // chunk,),
        in_specs=[
            pl.BlockSpec(wa.shape, lambda k: (0, 0)),
            pl.BlockSpec((xa.shape[0], chunk), lambda k: (0, k)),
            pl.BlockSpec(wb.shape, lambda k: (0, 0)),
            pl.BlockSpec((xb.shape[0], chunk), lambda k: (0, k)),
        ],
        out_specs=pl.BlockSpec((rows, chunk), lambda k: (0, k)),
        out_shape=jax.ShapeDtypeStruct((rows, pixels), jnp.bfloat16),
        cost_estimate=pl.CostEstimate(flops=flops, transcendentals=0, bytes_accessed=bytes_accessed),
    )(wa, xa, wb, xb)


def shards(particles, noise_prec, prior_pose, owners, projections, pose_index):
    f32 = jnp.float32
    count_dom = lax.axis_size("dom")
    count_ref = lax.axis_size("ref")
    arrived, pixels = particles.shape
    capacity = (5 * arrived + 4 * count_dom - 1) // (4 * count_dom)
    rows_a = min(FIRST_ROWS, capacity)
    rows_b = capacity - rows_a

    earlier = jnp.arange(arrived)[:, None] > jnp.arange(arrived)[None, :]
    same_owner = owners[:, None] == owners[None, :]
    slot_rank = jnp.sum(same_owner & earlier, axis=1).astype(jnp.int32)
    in_a = slot_rank < rows_a

    def pick(slot_of, count):
        return slot_of[None, :] == jnp.arange(count, dtype=jnp.int32)[:, None]

    pick_a = pick(jnp.where(in_a, owners * rows_a + slot_rank, -1), count_dom * rows_a)
    send_a = jnp.dot(pick_a.astype(particles.dtype), particles, preferred_element_type=f32)
    send_a = send_a.astype(particles.dtype).reshape(count_dom, rows_a, pixels)
    pick_all = pick(owners * capacity + slot_rank, count_dom * capacity)
    send_prec = jnp.sum(jnp.where(pick_all, noise_prec.astype(f32)[None, :], 0.0), axis=1)
    send_prior = jnp.sum(jnp.where(pick_all, prior_pose.astype(f32)[None, :] + 1.0, 0.0), axis=1) - 1.0
    meta = jnp.stack(
        [send_prec.reshape(count_dom, capacity), send_prior.reshape(count_dom, capacity)], axis=1
    )
    got_meta = lax.all_to_all(meta, "dom", 0, 0, tiled=True)
    got_a = lax.all_to_all(send_a, "dom", 0, 0, tiled=True).reshape(count_dom * rows_a, pixels)
    if rows_b:
        pick_b = pick(jnp.where(in_a, -1, owners * rows_b + slot_rank - rows_a), count_dom * rows_b)
        send_a, pick_b = lax.optimization_barrier((send_a, pick_b))
        send_b = jnp.dot(pick_b.astype(particles.dtype), particles, preferred_element_type=f32)
        send_b = send_b.astype(particles.dtype).reshape(count_dom, rows_b, pixels)
        got_a, send_b = lax.optimization_barrier((got_a, send_b))
        got_b = lax.all_to_all(send_b, "dom", 0, 0, tiled=True).reshape(count_dom * rows_b, pixels)

    own_proj = projections.reshape(-1, pixels)
    all_proj = lax.all_gather(own_proj, "ref", axis=0, tiled=True)
    rows = all_proj.shape[0]
    offsets = [u - SHIFTS // 2 for u in range(SHIFTS)]
    shifted = jnp.concatenate([translate(all_proj, -t) for t in offsets], axis=0)
    norms = jnp.sum(jnp.square(all_proj.astype(f32)), axis=1)
    per_class = projections.shape[1]
    pose_f = pose_index.astype(f32)

    def part(images, precision, prior_ids):
        n = images.shape[0]
        live = (prior_ids >= 0).astype(f32)
        corr = lax.dot_general(
            images, shifted, (((1,), (1,)), ((), ())), preferred_element_type=f32
        ).reshape(n, SHIFTS, rows)
        log_prior = -jnp.abs(pose_f[None, :] - prior_ids[:, None]) / PRIOR_WIDTH
        prior_rows = jnp.tile(log_prior, (1, rows // per_class))
        scaled = corr / IMG - norms[None, None, :] / (2.0 * IMG * IMG)
        scores = precision[:, None, None] * scaled + prior_rows[:, None, :]
        highest = jnp.max(scores, axis=(1, 2))
        loglike = highest + jnp.log(jnp.sum(jnp.exp(scores - highest[:, None, None]), axis=(1, 2)))
        weights = jnp.exp(scores - loglike[:, None, None]) * live[:, None, None]
        class_post = jnp.sum(weights.reshape(n, SHIFTS, rows // per_class, per_class), axis=(1, 3))
        totals = jnp.sum(weights, axis=(0, 1))
        low = weights.astype(jnp.bfloat16).reshape(n, SHIFTS * rows).T
        post = jnp.concatenate([class_post, loglike[:, None]], axis=1)
        return low, totals, post

    meta_prec = got_meta[:, 0, :]
    meta_prior = got_meta[:, 1, :]
    low_a, tot_a, post_a = part(
        got_a, meta_prec[:, :rows_a].reshape(-1), meta_prior[:, :rows_a].reshape(-1)
    )
    post_width = post_a.shape[1]
    back = [post_a.reshape(count_dom, rows_a, post_width)]
    if rows_b:
        low_b, tot_b, post_b = part(
            got_b, meta_prec[:, rows_a:].reshape(-1), meta_prior[:, rows_a:].reshape(-1)
        )
        tot_a = tot_a + tot_b
        back.append(post_b.reshape(count_dom, rows_b, post_width))
    back = jnp.concatenate(back, axis=1)
    got_back = lax.all_to_all(back, "dom", 0, 0, tiled=True).reshape(count_dom * capacity, post_width)

    if not rows_b:
        low_b = jnp.zeros((SHIFTS * rows, 8), jnp.bfloat16)
        got_b = jnp.zeros((8, pixels), particles.dtype)
    image_sums = class_image_sums(low_a, got_a, low_b, got_b, offsets)
    partial = image_sums.reshape(count_ref, rows // count_ref, pixels)
    got_partial = lax.all_to_all(partial, "ref", 0, 0, tiled=True)
    class_sums = jnp.sum(got_partial.astype(f32), axis=0).astype(jnp.bfloat16)
    class_sums = class_sums.reshape(projections.shape)
    got_tot = lax.all_to_all(tot_a.reshape(count_ref, rows // count_ref), "ref", 0, 0, tiled=True)
    weight_totals = jnp.sum(got_tot, axis=0).reshape(projections.shape[0], projections.shape[1])

    mine = got_back[owners * capacity + slot_rank]
    class_prob = mine[:, : post_width - 1]
    log_like = mine[:, post_width - 1]
    return (class_prob, log_like, class_sums, weight_totals)


def solution(mesh):
    in_specs = (
        P(("dom", "ref"), None),
        P(("dom", "ref")),
        P(("dom", "ref")),
        P(("dom", "ref")),
        P("ref", "dom", None),
        P("dom"),
    )
    out_specs = (P(("dom", "ref"), None), P(("dom", "ref")), P("ref", "dom", None), P("ref", "dom"))
    return jax.shard_map(shards, mesh=mesh, in_specs=in_specs, out_specs=out_specs, check_vma=False)
```

```python
import functools

import jax
import jax.numpy as jnp
from jax import lax
from jax.experimental import pallas as pl
from jax.experimental.pallas import tpu as pltpu
from jax.sharding import PartitionSpec as P

IMG = 128
SHIFTS = 3
PRIOR_WIDTH = 576
FIRST_ROWS = 8
CHUNK = 2048


def translate(images, offset):
    if offset == 0:
        return images
    pixels = images.shape[-1]
    lane = lax.broadcasted_iota(jnp.int32, images.shape, images.ndim - 1) % IMG
    near = jnp.roll(images, offset, axis=-1)
    if offset > 0:
        far = jnp.roll(images, offset - IMG, axis=-1)
        keep = lane >= offset
    else:
        far = jnp.roll(images, offset + IMG, axis=-1)
        keep = lane < IMG + offset
    del pixels
    return jnp.where(keep, near, far)


def rolled_sum(y, rows, offsets, lanes):
    acc = None
    for u, t in enumerate(offsets):
        blk = y[u * rows:(u + 1) * rows, lanes * IMG:(lanes + 1) * IMG]
        if t % IMG:
            blk = pltpu.roll(blk, shift=t % IMG, axis=1)
        acc = blk if acc is None else acc + blk
    return acc


def first_sums_kernel(offsets, rows, w_ref, x_ref, out_ref):
    y = jnp.dot(w_ref[...], x_ref[...], preferred_element_type=jnp.float32)
    for j in range(out_ref.shape[1] // IMG):
        out_ref[:, j * IMG:(j + 1) * IMG] = rolled_sum(y, rows, offsets, j)


def last_sums_kernel(offsets, rows, chunk, w_ref, x_ref, acc_ref, tail_ref, out_ref):
    k = pl.program_id(0)
    y = jnp.dot(w_ref[...], x_ref[...], preferred_element_type=jnp.float32)
    for j in range(chunk // IMG):
        total = acc_ref[:, j * IMG:(j + 1) * IMG] + rolled_sum(y, rows, offsets, j)
        out_ref[:, pl.ds(k * chunk + j * IMG, IMG)] = total.astype(out_ref.dtype)
    pixels = out_ref.shape[1] - tail_ref.shape[1]
    out_ref[:, pixels:] = tail_ref[...]


def first_sums(w, x, offsets):
    rows = w.shape[0] // len(offsets)
    pixels = x.shape[1]
    chunk = min(CHUNK, pixels)
    return pl.pallas_call(
        functools.partial(first_sums_kernel, tuple(offsets), rows),
        grid=(pixels // chunk,),
        in_specs=[
            pl.BlockSpec(w.shape, lambda k: (0, 0)),
            pl.BlockSpec((x.shape[0], chunk), lambda k: (0, k)),
        ],
        out_specs=pl.BlockSpec((rows, chunk), lambda k: (0, k)),
        out_shape=jax.ShapeDtypeStruct((rows, pixels), jnp.float32),
        cost_estimate=pl.CostEstimate(
            flops=2 * w.shape[0] * pixels * x.shape[0],
            transcendentals=0,
            bytes_accessed=2 * (x.size + w.size) + 4 * rows * pixels,
        ),
    )(w, x)


def last_sums(w, x, acc, tail, offsets):
    rows = w.shape[0] // len(offsets)
    pixels = x.shape[1]
    chunk = min(CHUNK, pixels)
    width = pixels + tail.shape[1]
    return pl.pallas_call(
        functools.partial(last_sums_kernel, tuple(offsets), rows, chunk),
        grid=(pixels // chunk,),
        in_specs=[
            pl.BlockSpec(w.shape, lambda k: (0, 0)),
            pl.BlockSpec((x.shape[0], chunk), lambda k: (0, k)),
            pl.BlockSpec((rows, chunk), lambda k: (0, k)),
            pl.BlockSpec(tail.shape, lambda k: (0, 0)),
        ],
        out_specs=pl.BlockSpec((rows, width), lambda k: (0, 0)),
        out_shape=jax.ShapeDtypeStruct((rows, width), jnp.bfloat16),
        cost_estimate=pl.CostEstimate(
            flops=2 * w.shape[0] * pixels * x.shape[0],
            transcendentals=0,
            bytes_accessed=2 * (x.size + w.size + rows * width) + 4 * rows * pixels,
        ),
    )(w, x, acc, tail)


def split_bf16(values):
    hi = values.astype(jnp.bfloat16)
    rest = values - hi.astype(jnp.float32)
    mid = rest.astype(jnp.bfloat16)
    lo = (rest - mid.astype(jnp.float32)).astype(jnp.bfloat16)
    return [hi, mid, lo]


def shards(particles, noise_prec, prior_pose, owners, projections, pose_index):
    f32 = jnp.float32
    count_dom = lax.axis_size("dom")
    count_ref = lax.axis_size("ref")
    arrived, pixels = particles.shape
    capacity = (5 * arrived + 4 * count_dom - 1) // (4 * count_dom)
    rows_a = min(FIRST_ROWS, capacity)
    rows_b = capacity - rows_a

    earlier = jnp.arange(arrived)[:, None] > jnp.arange(arrived)[None, :]
    same_owner = owners[:, None] == owners[None, :]
    slot_rank = jnp.sum(same_owner & earlier, axis=1).astype(jnp.int32)
    in_a = slot_rank < rows_a

    def pick(slot_of, count):
        return slot_of[None, :] == jnp.arange(count, dtype=jnp.int32)[:, None]

    pick_a = pick(jnp.where(in_a, owners * rows_a + slot_rank, -1), count_dom * rows_a)
    send_a = jnp.dot(pick_a.astype(particles.dtype), particles, preferred_element_type=f32)
    send_a = send_a.astype(particles.dtype).reshape(count_dom, rows_a, pixels)
    pick_all = pick(owners * capacity + slot_rank, count_dom * capacity)
    send_prec = jnp.sum(jnp.where(pick_all, noise_prec.astype(f32)[None, :], 0.0), axis=1)
    send_prior = jnp.sum(jnp.where(pick_all, prior_pose.astype(f32)[None, :] + 1.0, 0.0), axis=1) - 1.0
    meta = jnp.stack(
        [send_prec.reshape(count_dom, capacity), send_prior.reshape(count_dom, capacity)], axis=1
    )
    got_meta = lax.all_to_all(meta, "dom", 0, 0, tiled=True)
    got_a = lax.all_to_all(send_a, "dom", 0, 0, tiled=True).reshape(count_dom * rows_a, pixels)
    if rows_b:
        pick_b = pick(jnp.where(in_a, -1, owners * rows_b + slot_rank - rows_a), count_dom * rows_b)
        send_a, pick_b = lax.optimization_barrier((send_a, pick_b))
        send_b = jnp.dot(pick_b.astype(particles.dtype), particles, preferred_element_type=f32)
        send_b = send_b.astype(particles.dtype).reshape(count_dom, rows_b, pixels)
        got_a, send_b = lax.optimization_barrier((got_a, send_b))
        got_b = lax.all_to_all(send_b, "dom", 0, 0, tiled=True).reshape(count_dom * rows_b, pixels)

    own_proj = projections.reshape(-1, pixels)
    spread = jnp.broadcast_to(own_proj[None], (count_ref,) + own_proj.shape)
    all_proj = lax.all_to_all(spread, "ref", 0, 0, tiled=True).reshape(-1, pixels)
    rows = all_proj.shape[0]
    offsets = [u - SHIFTS // 2 for u in range(SHIFTS)]
    shifted = jnp.concatenate([translate(all_proj, -t) for t in offsets], axis=0)
    norms = jnp.sum(jnp.square(all_proj.astype(f32)), axis=1)
    per_class = projections.shape[1]
    pose_f = pose_index.astype(f32)

    def part(images, precision, prior_ids):
        n = images.shape[0]
        live = (prior_ids >= 0).astype(f32)
        corr = lax.dot_general(
            images, shifted, (((1,), (1,)), ((), ())), preferred_element_type=f32
        ).reshape(n, SHIFTS, rows)
        log_prior = -jnp.abs(pose_f[None, :] - prior_ids[:, None]) / PRIOR_WIDTH
        prior_rows = jnp.tile(log_prior, (1, rows // per_class))
        scaled = corr / IMG - norms[None, None, :] / (2.0 * IMG * IMG)
        scores = precision[:, None, None] * scaled + prior_rows[:, None, :]
        highest = jnp.max(scores, axis=(1, 2))
        loglike = highest + jnp.log(jnp.sum(jnp.exp(scores - highest[:, None, None]), axis=(1, 2)))
        weights = jnp.exp(scores - loglike[:, None, None]) * live[:, None, None]
        class_post = jnp.sum(weights.reshape(n, SHIFTS, rows // per_class, per_class), axis=(1, 3))
        totals = jnp.sum(weights, axis=(0, 1))
        low = weights.astype(jnp.bfloat16).reshape(n, SHIFTS * rows).T
        post = jnp.concatenate([class_post, loglike[:, None]], axis=1)
        return low, totals, post

    meta_prec = got_meta[:, 0, :]
    meta_prior = got_meta[:, 1, :]
    low_a, tot_a, post_a = part(
        got_a, meta_prec[:, :rows_a].reshape(-1), meta_prior[:, :rows_a].reshape(-1)
    )
    sums_a = first_sums(low_a, got_a, offsets)
    post_width = post_a.shape[1]
    back = [post_a.reshape(count_dom, rows_a, post_width)]
    if rows_b:
        low_b, tot_b, post_b = part(
            got_b, meta_prec[:, rows_a:].reshape(-1), meta_prior[:, rows_a:].reshape(-1)
        )
        tot_a = tot_a + tot_b
        back.append(post_b.reshape(count_dom, rows_b, post_width))
    back = jnp.concatenate(back, axis=1)
    got_back = lax.all_to_all(back, "dom", 0, 0, tiled=True).reshape(count_dom * capacity, post_width)

    if not rows_b:
        low_b = jnp.zeros((SHIFTS * rows, 8), jnp.bfloat16)
        got_b = jnp.zeros((8, pixels), particles.dtype)
    pieces = split_bf16(tot_a)
    tail = jnp.zeros((rows, IMG), jnp.bfloat16)
    for q, piece in enumerate(pieces):
        tail = tail.at[:, q].set(piece)
    image_sums = last_sums(low_b, got_b, sums_a, tail, offsets)
    partial = image_sums.reshape(count_ref, rows // count_ref, pixels + IMG)
    got_partial = lax.all_to_all(partial, "ref", 0, 0, tiled=True).astype(f32)
    class_sums = jnp.sum(got_partial[:, :, :pixels], axis=0).astype(jnp.bfloat16)
    class_sums = class_sums.reshape(projections.shape)
    got_tot = got_partial[:, :, pixels] + got_partial[:, :, pixels + 1] + got_partial[:, :, pixels + 2]
    weight_totals = jnp.sum(got_tot, axis=0).reshape(projections.shape[0], projections.shape[1])

    mine = got_back[owners * capacity + slot_rank]
    class_prob = mine[:, : post_width - 1]
    log_like = mine[:, post_width - 1]
    return (class_prob, log_like, class_sums, weight_totals)


def solution(mesh):
    in_specs = (
        P(("dom", "ref"), None),
        P(("dom", "ref")),
        P(("dom", "ref")),
        P(("dom", "ref")),
        P("ref", "dom", None),
        P("dom"),
    )
    out_specs = (P(("dom", "ref"), None), P(("dom", "ref")), P("ref", "dom", None), P("ref", "dom"))
    return jax.shard_map(shards, mesh=mesh, in_specs=in_specs, out_specs=out_specs, check_vma=False)
```

```python
import functools

import jax
import jax.numpy as jnp
from jax import lax
from jax.experimental import pallas as pl
from jax.experimental.pallas import tpu as pltpu
from jax.sharding import PartitionSpec as P

IMG = 128
SHIFTS = 3
PRIOR_WIDTH = 576
FIRST_ROWS = 8
CHUNK = 2048


def translate(images, offset):
    if offset == 0:
        return images
    pixels = images.shape[-1]
    lane = lax.broadcasted_iota(jnp.int32, images.shape, images.ndim - 1) % IMG
    near = jnp.roll(images, offset, axis=-1)
    if offset > 0:
        far = jnp.roll(images, offset - IMG, axis=-1)
        keep = lane >= offset
    else:
        far = jnp.roll(images, offset + IMG, axis=-1)
        keep = lane < IMG + offset
    del pixels
    return jnp.where(keep, near, far)


def rolled_sum(y, rows, offsets, lanes):
    acc = None
    for u, t in enumerate(offsets):
        blk = y[u * rows:(u + 1) * rows, lanes * IMG:(lanes + 1) * IMG]
        if t % IMG:
            blk = pltpu.roll(blk, shift=t % IMG, axis=1)
        acc = blk if acc is None else acc + blk
    return acc


def first_sums_kernel(offsets, rows, w_ref, x_ref, out_ref):
    y = jnp.dot(w_ref[...], x_ref[...], preferred_element_type=jnp.float32)
    for j in range(out_ref.shape[1] // IMG):
        out_ref[:, j * IMG:(j + 1) * IMG] = rolled_sum(y, rows, offsets, j)


def last_sums_kernel(offsets, rows, chunk, w_ref, x_ref, acc_ref, tail_ref, out_ref):
    k = pl.program_id(0)
    y = jnp.dot(w_ref[...], x_ref[...], preferred_element_type=jnp.float32)
    for j in range(chunk // IMG):
        total = acc_ref[:, j * IMG:(j + 1) * IMG] + rolled_sum(y, rows, offsets, j)
        out_ref[:, pl.ds(k * chunk + j * IMG, IMG)] = total.astype(out_ref.dtype)
    pixels = out_ref.shape[1] - tail_ref.shape[1]
    out_ref[:, pixels:] = tail_ref[...]


def first_sums(w, x, offsets):
    rows = w.shape[0] // len(offsets)
    pixels = x.shape[1]
    chunk = min(CHUNK, pixels)
    return pl.pallas_call(
        functools.partial(first_sums_kernel, tuple(offsets), rows),
        grid=(pixels // chunk,),
        in_specs=[
            pl.BlockSpec(w.shape, lambda k: (0, 0)),
            pl.BlockSpec((x.shape[0], chunk), lambda k: (0, k)),
        ],
        out_specs=pl.BlockSpec((rows, chunk), lambda k: (0, k)),
        out_shape=jax.ShapeDtypeStruct((rows, pixels), jnp.float32),
        cost_estimate=pl.CostEstimate(
            flops=2 * w.shape[0] * pixels * x.shape[0],
            transcendentals=0,
            bytes_accessed=2 * (x.size + w.size) + 4 * rows * pixels,
        ),
    )(w, x)


def last_sums(w, x, acc, tail, offsets):
    rows = w.shape[0] // len(offsets)
    pixels = x.shape[1]
    chunk = min(CHUNK, pixels)
    width = pixels + tail.shape[1]
    return pl.pallas_call(
        functools.partial(last_sums_kernel, tuple(offsets), rows, chunk),
        grid=(pixels // chunk,),
        in_specs=[
            pl.BlockSpec(w.shape, lambda k: (0, 0)),
            pl.BlockSpec((x.shape[0], chunk), lambda k: (0, k)),
            pl.BlockSpec((rows, chunk), lambda k: (0, k)),
            pl.BlockSpec(tail.shape, lambda k: (0, 0)),
        ],
        out_specs=pl.BlockSpec((rows, width), lambda k: (0, 0)),
        out_shape=jax.ShapeDtypeStruct((rows, width), jnp.bfloat16),
        cost_estimate=pl.CostEstimate(
            flops=2 * w.shape[0] * pixels * x.shape[0],
            transcendentals=0,
            bytes_accessed=2 * (x.size + w.size + rows * width) + 4 * rows * pixels,
        ),
    )(w, x, acc, tail)


def split_bf16(values):
    hi = values.astype(jnp.bfloat16)
    rest = values - hi.astype(jnp.float32)
    mid = rest.astype(jnp.bfloat16)
    lo = (rest - mid.astype(jnp.float32)).astype(jnp.bfloat16)
    return [hi, mid, lo]


def ahead(block, axis, distance):
    size = lax.axis_size(axis)
    return lax.ppermute(block, axis, [(i, (i + distance) % size) for i in range(size)])


def shards(particles, noise_prec, prior_pose, owners, projections, pose_index):
    f32 = jnp.float32
    count_dom = lax.axis_size("dom")
    count_ref = lax.axis_size("ref")
    arrived, pixels = particles.shape
    capacity = (5 * arrived + 4 * count_dom - 1) // (4 * count_dom)
    rows_a = min(FIRST_ROWS, capacity)
    rows_b = capacity - rows_a

    earlier = jnp.arange(arrived)[:, None] > jnp.arange(arrived)[None, :]
    same_owner = owners[:, None] == owners[None, :]
    slot_rank = jnp.sum(same_owner & earlier, axis=1).astype(jnp.int32)
    in_a = slot_rank < rows_a

    def pick(slot_of, count):
        return slot_of[None, :] == jnp.arange(count, dtype=jnp.int32)[:, None]

    pick_a = pick(jnp.where(in_a, owners * rows_a + slot_rank, -1), count_dom * rows_a)
    send_a = jnp.dot(pick_a.astype(particles.dtype), particles, preferred_element_type=f32)
    send_a = send_a.astype(particles.dtype).reshape(count_dom, rows_a, pixels)
    pick_all = pick(owners * capacity + slot_rank, count_dom * capacity)
    send_prec = jnp.sum(jnp.where(pick_all, noise_prec.astype(f32)[None, :], 0.0), axis=1)
    send_prior = jnp.sum(jnp.where(pick_all, prior_pose.astype(f32)[None, :] + 1.0, 0.0), axis=1) - 1.0
    meta = jnp.stack(
        [send_prec.reshape(count_dom, capacity), send_prior.reshape(count_dom, capacity)], axis=1
    )
    got_meta = lax.all_to_all(meta, "dom", 0, 0, tiled=True)
    got_a = lax.all_to_all(send_a, "dom", 0, 0, tiled=True).reshape(count_dom * rows_a, pixels)
    if rows_b:
        pick_b = pick(jnp.where(in_a, -1, owners * rows_b + slot_rank - rows_a), count_dom * rows_b)
        send_a, pick_b = lax.optimization_barrier((send_a, pick_b))
        send_b = jnp.dot(pick_b.astype(particles.dtype), particles, preferred_element_type=f32)
        send_b = send_b.astype(particles.dtype).reshape(count_dom, rows_b, pixels)
        got_a, send_b = lax.optimization_barrier((got_a, send_b))
        got_b = lax.all_to_all(send_b, "dom", 0, 0, tiled=True).reshape(count_dom * rows_b, pixels)

    own_proj = projections.reshape(-1, pixels)
    ref_here = lax.axis_index("ref")
    blocks = jnp.zeros((count_ref,) + own_proj.shape, own_proj.dtype)
    blocks = lax.dynamic_update_index_in_dim(blocks, own_proj, ref_here, 0)
    for k in range(1, count_ref):
        moved = ahead(own_proj, "ref", k)
        blocks = lax.dynamic_update_index_in_dim(blocks, moved, (ref_here - k) % count_ref, 0)
    all_proj = blocks.reshape(-1, pixels)
    rows = all_proj.shape[0]
    offsets = [u - SHIFTS // 2 for u in range(SHIFTS)]
    shifted = jnp.concatenate([translate(all_proj, -t) for t in offsets], axis=0)
    norms = jnp.sum(jnp.square(all_proj.astype(f32)), axis=1)
    per_class = projections.shape[1]
    pose_f = pose_index.astype(f32)

    def part(images, precision, prior_ids):
        n = images.shape[0]
        live = (prior_ids >= 0).astype(f32)
        corr = lax.dot_general(
            images, shifted, (((1,), (1,)), ((), ())), preferred_element_type=f32
        ).reshape(n, SHIFTS, rows)
        log_prior = -jnp.abs(pose_f[None, :] - prior_ids[:, None]) / PRIOR_WIDTH
        prior_rows = jnp.tile(log_prior, (1, rows // per_class))
        scaled = corr / IMG - norms[None, None, :] / (2.0 * IMG * IMG)
        scores = precision[:, None, None] * scaled + prior_rows[:, None, :]
        highest = jnp.max(scores, axis=(1, 2))
        loglike = highest + jnp.log(jnp.sum(jnp.exp(scores - highest[:, None, None]), axis=(1, 2)))
        weights = jnp.exp(scores - loglike[:, None, None]) * live[:, None, None]
        class_post = jnp.sum(weights.reshape(n, SHIFTS, rows // per_class, per_class), axis=(1, 3))
        totals = jnp.sum(weights, axis=(0, 1))
        low = weights.astype(jnp.bfloat16).reshape(n, SHIFTS * rows).T
        post = jnp.concatenate([class_post, loglike[:, None]], axis=1)
        return low, totals, post

    meta_prec = got_meta[:, 0, :]
    meta_prior = got_meta[:, 1, :]
    low_a, tot_a, post_a = part(
        got_a, meta_prec[:, :rows_a].reshape(-1), meta_prior[:, :rows_a].reshape(-1)
    )
    sums_a = first_sums(low_a, got_a, offsets)
    post_width = post_a.shape[1]
    back = [post_a.reshape(count_dom, rows_a, post_width)]
    if rows_b:
        low_b, tot_b, post_b = part(
            got_b, meta_prec[:, rows_a:].reshape(-1), meta_prior[:, rows_a:].reshape(-1)
        )
        tot_a = tot_a + tot_b
        back.append(post_b.reshape(count_dom, rows_b, post_width))
    back = jnp.concatenate(back, axis=1)
    got_back = lax.all_to_all(back, "dom", 0, 0, tiled=True).reshape(count_dom * capacity, post_width)

    if not rows_b:
        low_b = jnp.zeros((SHIFTS * rows, 8), jnp.bfloat16)
        got_b = jnp.zeros((8, pixels), particles.dtype)
    pieces = split_bf16(tot_a)
    tail = jnp.zeros((rows, IMG), jnp.bfloat16)
    for q, piece in enumerate(pieces):
        tail = tail.at[:, q].set(piece)
    image_sums = last_sums(low_b, got_b, sums_a, tail, offsets)
    partial = image_sums.reshape(count_ref, rows // count_ref, pixels + IMG)
    pieces = [lax.dynamic_index_in_dim(partial, ref_here, 0, keepdims=False)]
    for k in range(1, count_ref):
        outgoing = lax.dynamic_index_in_dim(partial, (ref_here + k) % count_ref, 0, keepdims=False)
        pieces.append(ahead(outgoing, "ref", k))
    got_partial = jnp.stack(pieces).astype(f32)
    class_sums = jnp.sum(got_partial[:, :, :pixels], axis=0).astype(jnp.bfloat16)
    class_sums = class_sums.reshape(projections.shape)
    got_tot = got_partial[:, :, pixels] + got_partial[:, :, pixels + 1] + got_partial[:, :, pixels + 2]
    weight_totals = jnp.sum(got_tot, axis=0).reshape(projections.shape[0], projections.shape[1])

    mine = got_back[owners * capacity + slot_rank]
    class_prob = mine[:, : post_width - 1]
    log_like = mine[:, post_width - 1]
    return (class_prob, log_like, class_sums, weight_totals)


def solution(mesh):
    in_specs = (
        P(("dom", "ref"), None),
        P(("dom", "ref")),
        P(("dom", "ref")),
        P(("dom", "ref")),
        P("ref", "dom", None),
        P("dom"),
    )
    out_specs = (P(("dom", "ref"), None), P(("dom", "ref")), P("ref", "dom", None), P("ref", "dom"))
    return jax.shard_map(shards, mesh=mesh, in_specs=in_specs, out_specs=out_specs, check_vma=False)
```

```python
import functools

import jax
import jax.numpy as jnp
from jax import lax
from jax.experimental import pallas as pl
from jax.experimental.pallas import tpu as pltpu
from jax.sharding import PartitionSpec as P

IMG = 128
SHIFTS = 3
PRIOR_WIDTH = 576
FIRST_ROWS = 8
CHUNK = 2048


def translate(images, offset):
    if offset == 0:
        return images
    pixels = images.shape[-1]
    lane = lax.broadcasted_iota(jnp.int32, images.shape, images.ndim - 1) % IMG
    near = jnp.roll(images, offset, axis=-1)
    if offset > 0:
        far = jnp.roll(images, offset - IMG, axis=-1)
        keep = lane >= offset
    else:
        far = jnp.roll(images, offset + IMG, axis=-1)
        keep = lane < IMG + offset
    del pixels
    return jnp.where(keep, near, far)


def rolled_sum(y, rows, offsets, lanes):
    acc = None
    for u, t in enumerate(offsets):
        blk = y[u * rows:(u + 1) * rows, lanes * IMG:(lanes + 1) * IMG]
        if t % IMG:
            blk = pltpu.roll(blk, shift=t % IMG, axis=1)
        acc = blk if acc is None else acc + blk
    return acc


def first_sums_kernel(offsets, rows, w_ref, x_ref, out_ref):
    y = jnp.dot(w_ref[...], x_ref[...], preferred_element_type=jnp.float32)
    for j in range(out_ref.shape[1] // IMG):
        out_ref[:, j * IMG:(j + 1) * IMG] = rolled_sum(y, rows, offsets, j)


def last_sums_kernel(offsets, rows, chunk, w_ref, x_ref, acc_ref, tail_ref, out_ref, moved_ref):
    k = pl.program_id(0)
    x = x_ref[...].astype(jnp.float32)
    total = acc_ref[...]
    for u, t in enumerate(offsets):
        if t % IMG:
            for j in range(chunk // IMG):
                piece = x[:, j * IMG:(j + 1) * IMG]
                moved_ref[:, j * IMG:(j + 1) * IMG] = pltpu.roll(piece, shift=t % IMG, axis=1).astype(
                    moved_ref.dtype
                )
            shifted_x = moved_ref[...]
        else:
            shifted_x = x_ref[...]
        w = w_ref[u * rows:(u + 1) * rows, :]
        total = total + jnp.dot(w, shifted_x, preferred_element_type=jnp.float32)
    out_ref[:, pl.ds(k * chunk, chunk)] = total.astype(out_ref.dtype)
    pixels = out_ref.shape[1] - tail_ref.shape[1]
    out_ref[:, pixels:] = tail_ref[...]


def first_sums(w, x, offsets):
    rows = w.shape[0] // len(offsets)
    pixels = x.shape[1]
    chunk = min(CHUNK, pixels)
    return pl.pallas_call(
        functools.partial(first_sums_kernel, tuple(offsets), rows),
        grid=(pixels // chunk,),
        in_specs=[
            pl.BlockSpec(w.shape, lambda k: (0, 0)),
            pl.BlockSpec((x.shape[0], chunk), lambda k: (0, k)),
        ],
        out_specs=pl.BlockSpec((rows, chunk), lambda k: (0, k)),
        out_shape=jax.ShapeDtypeStruct((rows, pixels), jnp.float32),
        cost_estimate=pl.CostEstimate(
            flops=2 * w.shape[0] * pixels * x.shape[0],
            transcendentals=0,
            bytes_accessed=2 * (x.size + w.size) + 4 * rows * pixels,
        ),
    )(w, x)


def last_sums(w, x, acc, tail, offsets):
    rows = w.shape[0] // len(offsets)
    pixels = x.shape[1]
    chunk = min(CHUNK, pixels)
    width = pixels + tail.shape[1]
    return pl.pallas_call(
        functools.partial(last_sums_kernel, tuple(offsets), rows, chunk),
        grid=(pixels // chunk,),
        in_specs=[
            pl.BlockSpec(w.shape, lambda k: (0, 0)),
            pl.BlockSpec((x.shape[0], chunk), lambda k: (0, k)),
            pl.BlockSpec((rows, chunk), lambda k: (0, k)),
            pl.BlockSpec(tail.shape, lambda k: (0, 0)),
        ],
        out_specs=pl.BlockSpec((rows, width), lambda k: (0, 0)),
        out_shape=jax.ShapeDtypeStruct((rows, width), jnp.bfloat16),
        scratch_shapes=[pltpu.VMEM((x.shape[0], chunk), x.dtype)],
        cost_estimate=pl.CostEstimate(
            flops=2 * w.shape[0] * pixels * x.shape[0],
            transcendentals=0,
            bytes_accessed=2 * (x.size + w.size + rows * width) + 4 * rows * pixels,
        ),
    )(w, x, acc, tail)


def split_bf16(values):
    hi = values.astype(jnp.bfloat16)
    rest = values - hi.astype(jnp.float32)
    mid = rest.astype(jnp.bfloat16)
    lo = (rest - mid.astype(jnp.float32)).astype(jnp.bfloat16)
    return [hi, mid, lo]


def ahead(block, axis, distance):
    size = lax.axis_size(axis)
    return lax.ppermute(block, axis, [(i, (i + distance) % size) for i in range(size)])


def shards(particles, noise_prec, prior_pose, owners, projections, pose_index):
    f32 = jnp.float32
    count_dom = lax.axis_size("dom")
    count_ref = lax.axis_size("ref")
    arrived, pixels = particles.shape
    capacity = (5 * arrived + 4 * count_dom - 1) // (4 * count_dom)
    rows_a = min(FIRST_ROWS, capacity)
    rows_b = capacity - rows_a

    earlier = jnp.arange(arrived)[:, None] > jnp.arange(arrived)[None, :]
    same_owner = owners[:, None] == owners[None, :]
    slot_rank = jnp.sum(same_owner & earlier, axis=1).astype(jnp.int32)
    in_a = slot_rank < rows_a

    def pick(slot_of, count):
        return slot_of[None, :] == jnp.arange(count, dtype=jnp.int32)[:, None]

    pick_a = pick(jnp.where(in_a, owners * rows_a + slot_rank, -1), count_dom * rows_a)
    send_a = jnp.dot(pick_a.astype(particles.dtype), particles, preferred_element_type=f32)
    send_a = send_a.astype(particles.dtype).reshape(count_dom, rows_a, pixels)
    pick_all = pick(owners * capacity + slot_rank, count_dom * capacity)
    send_prec = jnp.sum(jnp.where(pick_all, noise_prec.astype(f32)[None, :], 0.0), axis=1)
    send_prior = jnp.sum(jnp.where(pick_all, prior_pose.astype(f32)[None, :] + 1.0, 0.0), axis=1) - 1.0
    meta = jnp.stack(
        [send_prec.reshape(count_dom, capacity), send_prior.reshape(count_dom, capacity)], axis=1
    )
    got_meta = lax.all_to_all(meta, "dom", 0, 0, tiled=True)
    got_a = lax.all_to_all(send_a, "dom", 0, 0, tiled=True).reshape(count_dom * rows_a, pixels)
    own_proj = projections.reshape(-1, pixels)
    ref_here = lax.axis_index("ref")
    blocks = jnp.zeros((count_ref,) + own_proj.shape, own_proj.dtype)
    blocks = lax.dynamic_update_index_in_dim(blocks, own_proj, ref_here, 0)
    for k in range(1, count_ref):
        moved = ahead(own_proj, "ref", k)
        blocks = lax.dynamic_update_index_in_dim(blocks, moved, (ref_here - k) % count_ref, 0)
    all_proj = blocks.reshape(-1, pixels)
    if rows_b:
        pick_b = pick(jnp.where(in_a, -1, owners * rows_b + slot_rank - rows_a), count_dom * rows_b)
        all_proj, pick_b = lax.optimization_barrier((all_proj, pick_b))
        send_b = jnp.dot(pick_b.astype(particles.dtype), particles, preferred_element_type=f32)
        send_b = send_b.astype(particles.dtype).reshape(count_dom, rows_b, pixels)
        got_a, send_b = lax.optimization_barrier((got_a, send_b))
        got_b = lax.all_to_all(send_b, "dom", 0, 0, tiled=True).reshape(count_dom * rows_b, pixels)

    rows = all_proj.shape[0]
    offsets = [u - SHIFTS // 2 for u in range(SHIFTS)]
    shifted = jnp.concatenate([translate(all_proj, -t) for t in offsets], axis=0)
    norms = jnp.sum(jnp.square(all_proj.astype(f32)), axis=1)
    per_class = projections.shape[1]
    pose_f = pose_index.astype(f32)

    def part(images, precision, prior_ids):
        n = images.shape[0]
        live = (prior_ids >= 0).astype(f32)
        corr = lax.dot_general(
            images, shifted, (((1,), (1,)), ((), ())), preferred_element_type=f32
        ).reshape(n, SHIFTS, rows)
        log_prior = -jnp.abs(pose_f[None, :] - prior_ids[:, None]) / PRIOR_WIDTH
        prior_rows = jnp.tile(log_prior, (1, rows // per_class))
        scaled = corr / IMG - norms[None, None, :] / (2.0 * IMG * IMG)
        scores = precision[:, None, None] * scaled + prior_rows[:, None, :]
        highest = jnp.max(scores, axis=(1, 2))
        loglike = highest + jnp.log(jnp.sum(jnp.exp(scores - highest[:, None, None]), axis=(1, 2)))
        weights = jnp.exp(scores - loglike[:, None, None]) * live[:, None, None]
        class_post = jnp.sum(weights.reshape(n, SHIFTS, rows // per_class, per_class), axis=(1, 3))
        totals = jnp.sum(weights, axis=(0, 1))
        low = weights.astype(jnp.bfloat16).reshape(n, SHIFTS * rows).T
        post = jnp.concatenate([class_post, loglike[:, None]], axis=1)
        return low, totals, post

    meta_prec = got_meta[:, 0, :]
    meta_prior = got_meta[:, 1, :]
    low_a, tot_a, post_a = part(
        got_a, meta_prec[:, :rows_a].reshape(-1), meta_prior[:, :rows_a].reshape(-1)
    )
    sums_a = first_sums(low_a, got_a, offsets)
    post_width = post_a.shape[1]
    back = [post_a.reshape(count_dom, rows_a, post_width)]
    if rows_b:
        low_b, tot_b, post_b = part(
            got_b, meta_prec[:, rows_a:].reshape(-1), meta_prior[:, rows_a:].reshape(-1)
        )
        tot_a = tot_a + tot_b
        back.append(post_b.reshape(count_dom, rows_b, post_width))
    back = jnp.concatenate(back, axis=1)
    got_back = lax.all_to_all(back, "dom", 0, 0, tiled=True).reshape(count_dom * capacity, post_width)

    if not rows_b:
        low_b = jnp.zeros((SHIFTS * rows, 8), jnp.bfloat16)
        got_b = jnp.zeros((8, pixels), particles.dtype)
    pieces = split_bf16(tot_a)
    tail = jnp.zeros((rows, IMG), jnp.bfloat16)
    for q, piece in enumerate(pieces):
        tail = tail.at[:, q].set(piece)
    image_sums = last_sums(low_b, got_b, sums_a, tail, offsets)
    partial = image_sums.reshape(count_ref, rows // count_ref, pixels + IMG)
    pieces = [lax.dynamic_index_in_dim(partial, ref_here, 0, keepdims=False)]
    for k in range(1, count_ref):
        outgoing = lax.dynamic_index_in_dim(partial, (ref_here + k) % count_ref, 0, keepdims=False)
        pieces.append(ahead(outgoing, "ref", k))
    got_partial = jnp.stack(pieces).astype(f32)
    class_sums = jnp.sum(got_partial[:, :, :pixels], axis=0).astype(jnp.bfloat16)
    class_sums = class_sums.reshape(projections.shape)
    got_tot = got_partial[:, :, pixels] + got_partial[:, :, pixels + 1] + got_partial[:, :, pixels + 2]
    weight_totals = jnp.sum(got_tot, axis=0).reshape(projections.shape[0], projections.shape[1])

    mine = got_back[owners * capacity + slot_rank]
    class_prob = mine[:, : post_width - 1]
    log_like = mine[:, post_width - 1]
    return (class_prob, log_like, class_sums, weight_totals)


def solution(mesh):
    in_specs = (
        P(("dom", "ref"), None),
        P(("dom", "ref")),
        P(("dom", "ref")),
        P(("dom", "ref")),
        P("ref", "dom", None),
        P("dom"),
    )
    out_specs = (P(("dom", "ref"), None), P(("dom", "ref")), P("ref", "dom", None), P("ref", "dom"))
    return jax.shard_map(shards, mesh=mesh, in_specs=in_specs, out_specs=out_specs, check_vma=False)
```

```python
import functools

import jax
import jax.numpy as jnp
from jax import lax
from jax.experimental import pallas as pl
from jax.experimental.pallas import tpu as pltpu
from jax.sharding import PartitionSpec as P

IMG = 128
SHIFTS = 3
PRIOR_WIDTH = 576
FIRST_ROWS = 8
CHUNK = 2048


def translate(images, offset):
    if offset == 0:
        return images
    pixels = images.shape[-1]
    lane = lax.broadcasted_iota(jnp.int32, images.shape, images.ndim - 1) % IMG
    near = jnp.roll(images, offset, axis=-1)
    if offset > 0:
        far = jnp.roll(images, offset - IMG, axis=-1)
        keep = lane >= offset
    else:
        far = jnp.roll(images, offset + IMG, axis=-1)
        keep = lane < IMG + offset
    del pixels
    return jnp.where(keep, near, far)


def rolled_sum(y, rows, offsets, lanes):
    acc = None
    for u, t in enumerate(offsets):
        blk = y[u * rows:(u + 1) * rows, lanes * IMG:(lanes + 1) * IMG]
        if t % IMG:
            blk = pltpu.roll(blk, shift=t % IMG, axis=1)
        acc = blk if acc is None else acc + blk
    return acc


def first_sums_kernel(offsets, rows, w_ref, x_ref, out_ref):
    y = jnp.dot(w_ref[...], x_ref[...], preferred_element_type=jnp.float32)
    for j in range(out_ref.shape[1] // IMG):
        out_ref[:, j * IMG:(j + 1) * IMG] = rolled_sum(y, rows, offsets, j)


def last_sums_kernel(offsets, rows, chunk, w_ref, x_ref, acc_ref, tail_ref, out_ref, moved_ref):
    k = pl.program_id(0)
    x = x_ref[...].astype(jnp.float32)
    total = acc_ref[...]
    for u, t in enumerate(offsets):
        if t % IMG:
            for j in range(chunk // IMG):
                piece = x[:, j * IMG:(j + 1) * IMG]
                moved_ref[:, j * IMG:(j + 1) * IMG] = pltpu.roll(piece, shift=t % IMG, axis=1).astype(
                    moved_ref.dtype
                )
            shifted_x = moved_ref[...]
        else:
            shifted_x = x_ref[...]
        w = w_ref[u * rows:(u + 1) * rows, :]
        total = total + jnp.dot(w, shifted_x, preferred_element_type=jnp.float32)
    out_ref[:, pl.ds(k * chunk, chunk)] = total.astype(out_ref.dtype)
    pixels = out_ref.shape[1] - tail_ref.shape[1]
    out_ref[:, pixels:] = tail_ref[...]


def first_sums(w, x, offsets, pixels):
    rows = w.shape[0] // len(offsets)
    chunk = min(CHUNK, pixels)
    return pl.pallas_call(
        functools.partial(first_sums_kernel, tuple(offsets), rows),
        grid=(pixels // chunk,),
        in_specs=[
            pl.BlockSpec(w.shape, lambda k: (0, 0)),
            pl.BlockSpec((x.shape[0], chunk), lambda k: (0, k)),
        ],
        out_specs=pl.BlockSpec((rows, chunk), lambda k: (0, k)),
        out_shape=jax.ShapeDtypeStruct((rows, pixels), jnp.float32),
        cost_estimate=pl.CostEstimate(
            flops=2 * w.shape[0] * pixels * x.shape[0],
            transcendentals=0,
            bytes_accessed=2 * (x.shape[0] * pixels + w.size) + 4 * rows * pixels,
        ),
    )(w, x)


def last_sums(w, x, acc, tail, offsets, pixels):
    rows = w.shape[0] // len(offsets)
    chunk = min(CHUNK, pixels)
    width = pixels + tail.shape[1]
    return pl.pallas_call(
        functools.partial(last_sums_kernel, tuple(offsets), rows, chunk),
        grid=(pixels // chunk,),
        in_specs=[
            pl.BlockSpec(w.shape, lambda k: (0, 0)),
            pl.BlockSpec((x.shape[0], chunk), lambda k: (0, k)),
            pl.BlockSpec((rows, chunk), lambda k: (0, k)),
            pl.BlockSpec(tail.shape, lambda k: (0, 0)),
        ],
        out_specs=pl.BlockSpec((rows, width), lambda k: (0, 0)),
        out_shape=jax.ShapeDtypeStruct((rows, width), jnp.bfloat16),
        scratch_shapes=[pltpu.VMEM((x.shape[0], chunk), x.dtype)],
        cost_estimate=pl.CostEstimate(
            flops=2 * w.shape[0] * pixels * x.shape[0],
            transcendentals=0,
            bytes_accessed=2 * (x.shape[0] * pixels + w.size + rows * width) + 4 * rows * pixels,
        ),
    )(w, x, acc, tail)


def split_bf16(values):
    hi = values.astype(jnp.bfloat16)
    rest = values - hi.astype(jnp.float32)
    mid = rest.astype(jnp.bfloat16)
    lo = (rest - mid.astype(jnp.float32)).astype(jnp.bfloat16)
    return [hi, mid, lo]


def ahead(block, axis, distance):
    size = lax.axis_size(axis)
    return lax.ppermute(block, axis, [(i, (i + distance) % size) for i in range(size)])


def shards(particles, noise_prec, prior_pose, owners, projections, pose_index):
    f32 = jnp.float32
    count_dom = lax.axis_size("dom")
    count_ref = lax.axis_size("ref")
    arrived, pixels = particles.shape
    capacity = (5 * arrived + 4 * count_dom - 1) // (4 * count_dom)
    rows_a = min(FIRST_ROWS, capacity)
    rows_b = capacity - rows_a

    earlier = jnp.arange(arrived)[:, None] > jnp.arange(arrived)[None, :]
    same_owner = owners[:, None] == owners[None, :]
    slot_rank = jnp.sum(same_owner & earlier, axis=1).astype(jnp.int32)
    in_a = slot_rank < rows_a

    def pick(slot_of, count):
        return slot_of[None, :] == jnp.arange(count, dtype=jnp.int32)[:, None]

    code = prior_pose + 1
    lane = jnp.arange(IMG, dtype=jnp.int32)[None, :]
    extra = jnp.where(lane == 0, noise_prec.astype(f32)[:, None], 0.0)
    extra = jnp.where(lane == 1, (code // 64).astype(f32)[:, None], extra)
    extra = jnp.where(lane == 2, (code % 64).astype(f32)[:, None], extra)
    carried = jnp.concatenate([particles, extra.astype(particles.dtype)], axis=1)
    width = pixels + IMG

    pick_a = pick(jnp.where(in_a, owners * rows_a + slot_rank, -1), count_dom * rows_a)
    send_a = jnp.dot(pick_a.astype(particles.dtype), carried, preferred_element_type=f32)
    send_a = send_a.astype(particles.dtype).reshape(count_dom, rows_a, width)
    got_a = lax.all_to_all(send_a, "dom", 0, 0, tiled=True).reshape(count_dom * rows_a, width)
    own_proj = projections.reshape(-1, pixels)
    ref_here = lax.axis_index("ref")
    blocks = jnp.zeros((count_ref,) + own_proj.shape, own_proj.dtype)
    blocks = lax.dynamic_update_index_in_dim(blocks, own_proj, ref_here, 0)
    for k in range(1, count_ref):
        moved = ahead(own_proj, "ref", k)
        blocks = lax.dynamic_update_index_in_dim(blocks, moved, (ref_here - k) % count_ref, 0)
    all_proj = blocks.reshape(-1, pixels)
    if rows_b:
        pick_b = pick(jnp.where(in_a, -1, owners * rows_b + slot_rank - rows_a), count_dom * rows_b)
        all_proj, pick_b = lax.optimization_barrier((all_proj, pick_b))
        send_b = jnp.dot(pick_b.astype(particles.dtype), carried, preferred_element_type=f32)
        send_b = send_b.astype(particles.dtype).reshape(count_dom, rows_b, width)
        got_a, send_b = lax.optimization_barrier((got_a, send_b))
        got_b = lax.all_to_all(send_b, "dom", 0, 0, tiled=True).reshape(count_dom * rows_b, width)

    rows = all_proj.shape[0]
    offsets = [u - SHIFTS // 2 for u in range(SHIFTS)]
    shifted = jnp.concatenate([translate(all_proj, -t) for t in offsets], axis=0)
    norms = jnp.sum(jnp.square(all_proj.astype(f32)), axis=1)
    per_class = projections.shape[1]
    pose_f = pose_index.astype(f32)

    def part(received):
        n = received.shape[0]
        precision = received[:, pixels].astype(f32)
        prior_ids = received[:, pixels + 1].astype(f32) * 64.0 + received[:, pixels + 2].astype(f32) - 1.0
        live = (prior_ids >= 0).astype(f32)
        corr = lax.dot_general(
            received[:, :pixels], shifted, (((1,), (1,)), ((), ())), preferred_element_type=f32
        ).reshape(n, SHIFTS, rows)
        log_prior = -jnp.abs(pose_f[None, :] - prior_ids[:, None]) / PRIOR_WIDTH
        prior_rows = jnp.tile(log_prior, (1, rows // per_class))
        scaled = corr / IMG - norms[None, None, :] / (2.0 * IMG * IMG)
        scores = precision[:, None, None] * scaled + prior_rows[:, None, :]
        highest = jnp.max(scores, axis=(1, 2))
        loglike = highest + jnp.log(jnp.sum(jnp.exp(scores - highest[:, None, None]), axis=(1, 2)))
        weights = jnp.exp(scores - loglike[:, None, None]) * live[:, None, None]
        class_post = jnp.sum(weights.reshape(n, SHIFTS, rows // per_class, per_class), axis=(1, 3))
        totals = jnp.sum(weights, axis=(0, 1))
        low = weights.astype(jnp.bfloat16).reshape(n, SHIFTS * rows).T
        post = jnp.concatenate([class_post, loglike[:, None]], axis=1)
        return low, totals, post

    low_a, tot_a, post_a = part(got_a)
    sums_a = first_sums(low_a, got_a, offsets, pixels)
    post_width = post_a.shape[1]
    back = [post_a.reshape(count_dom, rows_a, post_width)]
    if rows_b:
        low_b, tot_b, post_b = part(got_b)
        tot_a = tot_a + tot_b
        back.append(post_b.reshape(count_dom, rows_b, post_width))
    back = jnp.concatenate(back, axis=1)
    got_back = lax.all_to_all(back, "dom", 0, 0, tiled=True).reshape(count_dom * capacity, post_width)

    if not rows_b:
        low_b = jnp.zeros((SHIFTS * rows, 8), jnp.bfloat16)
        got_b = jnp.zeros((8, width), particles.dtype)
    pieces = split_bf16(tot_a)
    tail = jnp.zeros((rows, IMG), jnp.bfloat16)
    for q, piece in enumerate(pieces):
        tail = tail.at[:, q].set(piece)
    image_sums = last_sums(low_b, got_b, sums_a, tail, offsets, pixels)
    partial = image_sums.reshape(count_ref, rows // count_ref, pixels + IMG)
    pieces = [lax.dynamic_index_in_dim(partial, ref_here, 0, keepdims=False)]
    for k in range(1, count_ref):
        outgoing = lax.dynamic_index_in_dim(partial, (ref_here + k) % count_ref, 0, keepdims=False)
        pieces.append(ahead(outgoing, "ref", k))
    got_partial = jnp.stack(pieces).astype(f32)
    class_sums = jnp.sum(got_partial[:, :, :pixels], axis=0).astype(jnp.bfloat16)
    class_sums = class_sums.reshape(projections.shape)
    got_tot = got_partial[:, :, pixels] + got_partial[:, :, pixels + 1] + got_partial[:, :, pixels + 2]
    weight_totals = jnp.sum(got_tot, axis=0).reshape(projections.shape[0], projections.shape[1])

    mine = got_back[owners * capacity + slot_rank]
    class_prob = mine[:, : post_width - 1]
    log_like = mine[:, post_width - 1]
    return (class_prob, log_like, class_sums, weight_totals)


def solution(mesh):
    in_specs = (
        P(("dom", "ref"), None),
        P(("dom", "ref")),
        P(("dom", "ref")),
        P(("dom", "ref")),
        P("ref", "dom", None),
        P("dom"),
    )
    out_specs = (P(("dom", "ref"), None), P(("dom", "ref")), P("ref", "dom", None), P("ref", "dom"))
    return jax.shard_map(shards, mesh=mesh, in_specs=in_specs, out_specs=out_specs, check_vma=False)
```

```python
import functools

import jax
import jax.numpy as jnp
from jax import lax
from jax.experimental import pallas as pl
from jax.experimental.pallas import tpu as pltpu
from jax.sharding import PartitionSpec as P

IMG = 128
SHIFTS = 3
PRIOR_WIDTH = 576
FIRST_ROWS = 8
CHUNK = 2048


def translate(images, offset):
    if offset == 0:
        return images
    pixels = images.shape[-1]
    lane = lax.broadcasted_iota(jnp.int32, images.shape, images.ndim - 1) % IMG
    near = jnp.roll(images, offset, axis=-1)
    if offset > 0:
        far = jnp.roll(images, offset - IMG, axis=-1)
        keep = lane >= offset
    else:
        far = jnp.roll(images, offset + IMG, axis=-1)
        keep = lane < IMG + offset
    del pixels
    return jnp.where(keep, near, far)


def rolled_sum(y, rows, offsets, lanes):
    acc = None
    for u, t in enumerate(offsets):
        blk = y[u * rows:(u + 1) * rows, lanes * IMG:(lanes + 1) * IMG]
        if t % IMG:
            blk = pltpu.roll(blk, shift=t % IMG, axis=1)
        acc = blk if acc is None else acc + blk
    return acc


def first_sums_kernel(offsets, rows, w_ref, x_ref, out_ref):
    y = jnp.dot(w_ref[...], x_ref[...], preferred_element_type=jnp.float32)
    for j in range(out_ref.shape[1] // IMG):
        out_ref[:, j * IMG:(j + 1) * IMG] = rolled_sum(y, rows, offsets, j)


def last_sums_kernel(offsets, rows, chunk, w_ref, x_ref, acc_ref, tail_ref, out_ref, moved_ref):
    k = pl.program_id(0)
    n = x_ref.shape[0]
    x = x_ref[:, pl.ds(k * chunk, chunk)]
    wide = x.astype(jnp.float32)
    for u, t in enumerate(offsets):
        if t % IMG:
            for j in range(chunk // IMG):
                piece = pltpu.roll(wide[:, j * IMG:(j + 1) * IMG], shift=t % IMG, axis=1)
                moved_ref[u * n:(u + 1) * n, j * IMG:(j + 1) * IMG] = piece.astype(moved_ref.dtype)
        else:
            moved_ref[u * n:(u + 1) * n, :] = x
    total = acc_ref[...] + jnp.dot(w_ref[...], moved_ref[...], preferred_element_type=jnp.float32)
    out_ref[:, pl.ds(k * chunk, chunk)] = total.astype(out_ref.dtype)
    pixels = out_ref.shape[1] - tail_ref.shape[1]
    out_ref[:, pixels:] = tail_ref[...]


def first_sums(w, x, offsets, pixels):
    rows = w.shape[0] // len(offsets)
    chunk = min(CHUNK, pixels)
    return pl.pallas_call(
        functools.partial(first_sums_kernel, tuple(offsets), rows),
        grid=(pixels // chunk,),
        in_specs=[
            pl.BlockSpec(w.shape, lambda k: (0, 0)),
            pl.BlockSpec((x.shape[0], chunk), lambda k: (0, k)),
        ],
        out_specs=pl.BlockSpec((rows, chunk), lambda k: (0, k)),
        out_shape=jax.ShapeDtypeStruct((rows, pixels), jnp.float32),
        cost_estimate=pl.CostEstimate(
            flops=2 * w.shape[0] * pixels * x.shape[0],
            transcendentals=0,
            bytes_accessed=2 * (x.shape[0] * pixels + w.size) + 4 * rows * pixels,
        ),
    )(w, x)


def last_sums(w, x, acc, tail, offsets, pixels):
    rows = acc.shape[0]
    chunk = min(CHUNK, pixels)
    width = pixels + tail.shape[1]
    n = x.shape[0]
    stacked_w = w.reshape(len(offsets), rows, n).transpose(1, 0, 2).reshape(rows, len(offsets) * n)
    return pl.pallas_call(
        functools.partial(last_sums_kernel, tuple(offsets), rows, chunk),
        grid=(pixels // chunk,),
        in_specs=[
            pl.BlockSpec(stacked_w.shape, lambda k: (0, 0)),
            pl.BlockSpec(x.shape, lambda k: (0, 0)),
            pl.BlockSpec((rows, chunk), lambda k: (0, k)),
            pl.BlockSpec(tail.shape, lambda k: (0, 0)),
        ],
        out_specs=pl.BlockSpec((rows, width), lambda k: (0, 0)),
        out_shape=jax.ShapeDtypeStruct((rows, width), jnp.bfloat16),
        scratch_shapes=[pltpu.VMEM((len(offsets) * n, chunk), x.dtype)],
        cost_estimate=pl.CostEstimate(
            flops=2 * w.shape[0] * pixels * n,
            transcendentals=0,
            bytes_accessed=2 * (n * width + w.size + rows * width) + 4 * rows * pixels,
        ),
    )(stacked_w, x, acc, tail)


def split_bf16(values):
    hi = values.astype(jnp.bfloat16)
    rest = values - hi.astype(jnp.float32)
    mid = rest.astype(jnp.bfloat16)
    lo = (rest - mid.astype(jnp.float32)).astype(jnp.bfloat16)
    return [hi, mid, lo]


def ahead(block, axis, distance):
    size = lax.axis_size(axis)
    return lax.ppermute(block, axis, [(i, (i + distance) % size) for i in range(size)])


def shards(particles, noise_prec, prior_pose, owners, projections, pose_index):
    f32 = jnp.float32
    count_dom = lax.axis_size("dom")
    count_ref = lax.axis_size("ref")
    arrived, pixels = particles.shape
    capacity = (5 * arrived + 4 * count_dom - 1) // (4 * count_dom)
    rows_a = min(FIRST_ROWS, capacity)
    rows_b = capacity - rows_a

    earlier = jnp.arange(arrived)[:, None] > jnp.arange(arrived)[None, :]
    same_owner = owners[:, None] == owners[None, :]
    slot_rank = jnp.sum(same_owner & earlier, axis=1).astype(jnp.int32)
    in_a = slot_rank < rows_a

    def pick(slot_of, count):
        return slot_of[None, :] == jnp.arange(count, dtype=jnp.int32)[:, None]

    code = prior_pose + 1
    lane = jnp.arange(IMG, dtype=jnp.int32)[None, :]
    extra = jnp.where(lane == 0, noise_prec.astype(f32)[:, None], 0.0)
    extra = jnp.where(lane == 1, (code // 64).astype(f32)[:, None], extra)
    extra = jnp.where(lane == 2, (code % 64).astype(f32)[:, None], extra)
    carried = jnp.concatenate([particles, extra.astype(particles.dtype)], axis=1)
    width = pixels + IMG

    pick_a = pick(jnp.where(in_a, owners * rows_a + slot_rank, -1), count_dom * rows_a)
    send_a = jnp.dot(pick_a.astype(particles.dtype), carried, preferred_element_type=f32)
    send_a = send_a.astype(particles.dtype).reshape(count_dom, rows_a, width)
    got_a = lax.all_to_all(send_a, "dom", 0, 0, tiled=True).reshape(count_dom * rows_a, width)
    _, own_proj = lax.optimization_barrier((send_a, projections.reshape(-1, pixels)))
    ref_here = lax.axis_index("ref")
    blocks = jnp.zeros((count_ref,) + own_proj.shape, own_proj.dtype)
    blocks = lax.dynamic_update_index_in_dim(blocks, own_proj, ref_here, 0)
    for k in range(1, count_ref):
        moved = ahead(own_proj, "ref", k)
        blocks = lax.dynamic_update_index_in_dim(blocks, moved, (ref_here - k) % count_ref, 0)
    all_proj = blocks.reshape(-1, pixels)
    if rows_b:
        pick_b = pick(jnp.where(in_a, -1, owners * rows_b + slot_rank - rows_a), count_dom * rows_b)
        all_proj, pick_b = lax.optimization_barrier((all_proj, pick_b))
        send_b = jnp.dot(pick_b.astype(particles.dtype), carried, preferred_element_type=f32)
        send_b = send_b.astype(particles.dtype).reshape(count_dom, rows_b, width)
        got_a, send_b = lax.optimization_barrier((got_a, send_b))
        got_b = lax.all_to_all(send_b, "dom", 0, 0, tiled=True).reshape(count_dom * rows_b, width)

    rows = all_proj.shape[0]
    offsets = [u - SHIFTS // 2 for u in range(SHIFTS)]
    shifted = jnp.concatenate([translate(all_proj, -t) for t in offsets], axis=0)
    norms = jnp.sum(jnp.square(all_proj.astype(f32)), axis=1)
    per_class = projections.shape[1]
    pose_f = pose_index.astype(f32)

    def part(received):
        n = received.shape[0]
        precision = received[:, pixels].astype(f32)
        prior_ids = received[:, pixels + 1].astype(f32) * 64.0 + received[:, pixels + 2].astype(f32) - 1.0
        live = (prior_ids >= 0).astype(f32)
        corr = lax.dot_general(
            received[:, :pixels], shifted, (((1,), (1,)), ((), ())), preferred_element_type=f32
        ).reshape(n, SHIFTS, rows)
        log_prior = -jnp.abs(pose_f[None, :] - prior_ids[:, None]) / PRIOR_WIDTH
        prior_rows = jnp.tile(log_prior, (1, rows // per_class))
        scaled = corr / IMG - norms[None, None, :] / (2.0 * IMG * IMG)
        scores = precision[:, None, None] * scaled + prior_rows[:, None, :]
        highest = jnp.max(scores, axis=(1, 2))
        loglike = highest + jnp.log(jnp.sum(jnp.exp(scores - highest[:, None, None]), axis=(1, 2)))
        weights = jnp.exp(scores - loglike[:, None, None]) * live[:, None, None]
        class_post = jnp.sum(weights.reshape(n, SHIFTS, rows // per_class, per_class), axis=(1, 3))
        totals = jnp.sum(weights, axis=(0, 1))
        low = weights.astype(jnp.bfloat16).reshape(n, SHIFTS * rows).T
        post = jnp.concatenate([class_post, loglike[:, None]], axis=1)
        return low, totals, post

    low_a, tot_a, post_a = part(got_a)
    sums_a = first_sums(low_a, got_a, offsets, pixels)
    post_width = post_a.shape[1]
    back = [post_a.reshape(count_dom, rows_a, post_width)]
    if rows_b:
        low_b, tot_b, post_b = part(got_b)
        tot_a = tot_a + tot_b
        back.append(post_b.reshape(count_dom, rows_b, post_width))
    back = jnp.concatenate(back, axis=1)
    got_back = lax.all_to_all(back, "dom", 0, 0, tiled=True).reshape(count_dom * capacity, post_width)

    if not rows_b:
        low_b = jnp.zeros((SHIFTS * rows, 8), jnp.bfloat16)
        got_b = jnp.zeros((8, width), particles.dtype)
    pieces = split_bf16(tot_a)
    tail = jnp.zeros((rows, IMG), jnp.bfloat16)
    for q, piece in enumerate(pieces):
        tail = tail.at[:, q].set(piece)
    image_sums = last_sums(low_b, got_b, sums_a, tail, offsets, pixels)
    partial = image_sums.reshape(count_ref, rows // count_ref, pixels + IMG)
    pieces = [lax.dynamic_index_in_dim(partial, ref_here, 0, keepdims=False)]
    for k in range(1, count_ref):
        outgoing = lax.dynamic_index_in_dim(partial, (ref_here + k) % count_ref, 0, keepdims=False)
        pieces.append(ahead(outgoing, "ref", k))
    got_partial = jnp.stack(pieces).astype(f32)
    class_sums = jnp.sum(got_partial[:, :, :pixels], axis=0).astype(jnp.bfloat16)
    class_sums = class_sums.reshape(projections.shape)
    got_tot = got_partial[:, :, pixels] + got_partial[:, :, pixels + 1] + got_partial[:, :, pixels + 2]
    weight_totals = jnp.sum(got_tot, axis=0).reshape(projections.shape[0], projections.shape[1])

    mine = got_back[owners * capacity + slot_rank]
    class_prob = mine[:, : post_width - 1]
    log_like = mine[:, post_width - 1]
    return (class_prob, log_like, class_sums, weight_totals)


def solution(mesh):
    in_specs = (
        P(("dom", "ref"), None),
        P(("dom", "ref")),
        P(("dom", "ref")),
        P(("dom", "ref")),
        P("ref", "dom", None),
        P("dom"),
    )
    out_specs = (P(("dom", "ref"), None), P(("dom", "ref")), P("ref", "dom", None), P("ref", "dom"))
    return jax.shard_map(shards, mesh=mesh, in_specs=in_specs, out_specs=out_specs, check_vma=False)
```

```python
import functools

import jax
import jax.numpy as jnp
from jax import lax
from jax.experimental import pallas as pl
from jax.experimental.pallas import tpu as pltpu
from jax.sharding import PartitionSpec as P

IMG = 128
SHIFTS = 3
PRIOR_WIDTH = 576
FIRST_ROWS = 8
CHUNK = 2048


def translate(images, offset):
    if offset == 0:
        return images
    pixels = images.shape[-1]
    lane = lax.broadcasted_iota(jnp.int32, images.shape, images.ndim - 1) % IMG
    near = jnp.roll(images, offset, axis=-1)
    if offset > 0:
        far = jnp.roll(images, offset - IMG, axis=-1)
        keep = lane >= offset
    else:
        far = jnp.roll(images, offset + IMG, axis=-1)
        keep = lane < IMG + offset
    del pixels
    return jnp.where(keep, near, far)


def rolled_sum(y, rows, offsets, lanes):
    acc = None
    for u, t in enumerate(offsets):
        blk = y[u * rows:(u + 1) * rows, lanes * IMG:(lanes + 1) * IMG]
        if t % IMG:
            blk = pltpu.roll(blk, shift=t % IMG, axis=1)
        acc = blk if acc is None else acc + blk
    return acc


def first_sums_kernel(offsets, rows, w_ref, x_ref, out_ref):
    y = jnp.dot(w_ref[...], x_ref[...], preferred_element_type=jnp.float32)
    for j in range(out_ref.shape[1] // IMG):
        out_ref[:, j * IMG:(j + 1) * IMG] = rolled_sum(y, rows, offsets, j)


def last_sums_kernel(offsets, rows, chunk, w_ref, x_ref, acc_ref, tail_ref, *refs):
    out_refs, moved_ref = refs[:-1], refs[-1]
    k = pl.program_id(0)
    n = x_ref.shape[0]
    x = x_ref[:, pl.ds(k * chunk, chunk)]
    wide = x.astype(jnp.float32)
    for u, t in enumerate(offsets):
        if t % IMG:
            for j in range(chunk // IMG):
                piece = pltpu.roll(wide[:, j * IMG:(j + 1) * IMG], shift=t % IMG, axis=1)
                moved_ref[u * n:(u + 1) * n, j * IMG:(j + 1) * IMG] = piece.astype(moved_ref.dtype)
        else:
            moved_ref[u * n:(u + 1) * n, :] = x
    total = acc_ref[...] + jnp.dot(w_ref[...], moved_ref[...], preferred_element_type=jnp.float32)
    group = rows // len(out_refs)
    for q, out_ref in enumerate(out_refs):
        pixels = out_ref.shape[1] - tail_ref.shape[1]
        out_ref[:, pl.ds(k * chunk, chunk)] = total[q * group:(q + 1) * group].astype(out_ref.dtype)
        out_ref[:, pixels:] = tail_ref[q * group:(q + 1) * group]


def first_sums(w, x, offsets, pixels):
    rows = w.shape[0] // len(offsets)
    chunk = min(CHUNK, pixels)
    return pl.pallas_call(
        functools.partial(first_sums_kernel, tuple(offsets), rows),
        grid=(pixels // chunk,),
        in_specs=[
            pl.BlockSpec(w.shape, lambda k: (0, 0)),
            pl.BlockSpec((x.shape[0], chunk), lambda k: (0, k)),
        ],
        out_specs=pl.BlockSpec((rows, chunk), lambda k: (0, k)),
        out_shape=jax.ShapeDtypeStruct((rows, pixels), jnp.float32),
        cost_estimate=pl.CostEstimate(
            flops=2 * w.shape[0] * pixels * x.shape[0],
            transcendentals=0,
            bytes_accessed=2 * (x.shape[0] * pixels + w.size) + 4 * rows * pixels,
        ),
    )(w, x)


def last_sums(w, x, acc, tail, offsets, pixels, blocks):
    rows = acc.shape[0]
    group = rows // blocks
    chunk = min(CHUNK, pixels)
    width = pixels + tail.shape[1]
    n = x.shape[0]
    stacked_w = w.reshape(len(offsets), rows, n).transpose(1, 0, 2).reshape(rows, len(offsets) * n)
    return pl.pallas_call(
        functools.partial(last_sums_kernel, tuple(offsets), rows, chunk),
        grid=(pixels // chunk,),
        in_specs=[
            pl.BlockSpec(stacked_w.shape, lambda k: (0, 0)),
            pl.BlockSpec(x.shape, lambda k: (0, 0)),
            pl.BlockSpec((rows, chunk), lambda k: (0, k)),
            pl.BlockSpec(tail.shape, lambda k: (0, 0)),
        ],
        out_specs=[pl.BlockSpec((group, width), lambda k: (0, 0)) for _ in range(blocks)],
        out_shape=[jax.ShapeDtypeStruct((group, width), jnp.bfloat16) for _ in range(blocks)],
        scratch_shapes=[pltpu.VMEM((len(offsets) * n, chunk), x.dtype)],
        cost_estimate=pl.CostEstimate(
            flops=2 * w.shape[0] * pixels * n,
            transcendentals=0,
            bytes_accessed=2 * (n * width + w.size + rows * width) + 4 * rows * pixels,
        ),
    )(stacked_w, x, acc, tail)


def split_bf16(values):
    hi = values.astype(jnp.bfloat16)
    rest = values - hi.astype(jnp.float32)
    mid = rest.astype(jnp.bfloat16)
    lo = (rest - mid.astype(jnp.float32)).astype(jnp.bfloat16)
    return [hi, mid, lo]


def ahead(block, axis, distance):
    size = lax.axis_size(axis)
    return lax.ppermute(block, axis, [(i, (i + distance) % size) for i in range(size)])


def shards(particles, noise_prec, prior_pose, owners, projections, pose_index):
    f32 = jnp.float32
    count_dom = lax.axis_size("dom")
    count_ref = lax.axis_size("ref")
    arrived, pixels = particles.shape
    capacity = (5 * arrived + 4 * count_dom - 1) // (4 * count_dom)
    rows_a = min(FIRST_ROWS, capacity)
    rows_b = capacity - rows_a

    earlier = jnp.arange(arrived)[:, None] > jnp.arange(arrived)[None, :]
    same_owner = owners[:, None] == owners[None, :]
    slot_rank = jnp.sum(same_owner & earlier, axis=1).astype(jnp.int32)
    in_a = slot_rank < rows_a

    def pick(slot_of, count):
        return slot_of[None, :] == jnp.arange(count, dtype=jnp.int32)[:, None]

    code = prior_pose + 1
    lane = jnp.arange(IMG, dtype=jnp.int32)[None, :]
    extra = jnp.where(lane == 0, noise_prec.astype(f32)[:, None], 0.0)
    extra = jnp.where(lane == 1, (code // 64).astype(f32)[:, None], extra)
    extra = jnp.where(lane == 2, (code % 64).astype(f32)[:, None], extra)
    carried = jnp.concatenate([particles, extra.astype(particles.dtype)], axis=1)
    width = pixels + IMG

    pick_a = pick(jnp.where(in_a, owners * rows_a + slot_rank, -1), count_dom * rows_a)
    send_a = jnp.dot(pick_a.astype(particles.dtype), carried, preferred_element_type=f32)
    send_a = send_a.astype(particles.dtype).reshape(count_dom, rows_a, width)
    got_a = lax.all_to_all(send_a, "dom", 0, 0, tiled=True).reshape(count_dom * rows_a, width)
    _, own_proj = lax.optimization_barrier((send_a, projections.reshape(-1, pixels)))
    ref_here = lax.axis_index("ref")
    blocks = jnp.zeros((count_ref,) + own_proj.shape, own_proj.dtype)
    blocks = lax.dynamic_update_index_in_dim(blocks, own_proj, ref_here, 0)
    for k in range(1, count_ref):
        moved = ahead(own_proj, "ref", k)
        blocks = lax.dynamic_update_index_in_dim(blocks, moved, (ref_here - k) % count_ref, 0)
    all_proj = blocks.reshape(-1, pixels)
    if rows_b:
        pick_b = pick(jnp.where(in_a, -1, owners * rows_b + slot_rank - rows_a), count_dom * rows_b)
        all_proj, pick_b = lax.optimization_barrier((all_proj, pick_b))
        send_b = jnp.dot(pick_b.astype(particles.dtype), carried, preferred_element_type=f32)
        send_b = send_b.astype(particles.dtype).reshape(count_dom, rows_b, width)
        got_a, send_b = lax.optimization_barrier((got_a, send_b))
        got_b = lax.all_to_all(send_b, "dom", 0, 0, tiled=True).reshape(count_dom * rows_b, width)

    rows = all_proj.shape[0]
    offsets = [u - SHIFTS // 2 for u in range(SHIFTS)]
    shifted = jnp.concatenate([translate(all_proj, -t) for t in offsets], axis=0)
    norms = jnp.sum(jnp.square(all_proj.astype(f32)), axis=1)
    per_class = projections.shape[1]
    pose_f = pose_index.astype(f32)

    def part(received):
        n = received.shape[0]
        precision = received[:, pixels].astype(f32)
        prior_ids = received[:, pixels + 1].astype(f32) * 64.0 + received[:, pixels + 2].astype(f32) - 1.0
        live = (prior_ids >= 0).astype(f32)
        corr = lax.dot_general(
            received[:, :pixels], shifted, (((1,), (1,)), ((), ())), preferred_element_type=f32
        ).reshape(n, SHIFTS, rows)
        log_prior = -jnp.abs(pose_f[None, :] - prior_ids[:, None]) / PRIOR_WIDTH
        prior_rows = jnp.tile(log_prior, (1, rows // per_class))
        scaled = corr / IMG - norms[None, None, :] / (2.0 * IMG * IMG)
        scores = precision[:, None, None] * scaled + prior_rows[:, None, :]
        highest = jnp.max(scores, axis=(1, 2))
        loglike = highest + jnp.log(jnp.sum(jnp.exp(scores - highest[:, None, None]), axis=(1, 2)))
        weights = jnp.exp(scores - loglike[:, None, None]) * live[:, None, None]
        class_post = jnp.sum(weights.reshape(n, SHIFTS, rows // per_class, per_class), axis=(1, 3))
        totals = jnp.sum(weights, axis=(0, 1))
        low = weights.astype(jnp.bfloat16).reshape(n, SHIFTS * rows).T
        post = jnp.concatenate([class_post, loglike[:, None]], axis=1)
        return low, totals, post

    order = (ref_here + jnp.arange(count_ref, dtype=jnp.int32)) % count_ref

    def rotate_rows(values, lead):
        shape = values.shape
        grouped = values.reshape((lead, count_ref, -1) + shape[1:])
        return jnp.take(grouped, order, axis=1).reshape(shape)

    low_a, tot_a, post_a = part(got_a)
    low_a = rotate_rows(low_a, SHIFTS)
    sums_a = first_sums(low_a, got_a, offsets, pixels)
    post_width = post_a.shape[1]
    back = [post_a.reshape(count_dom, rows_a, post_width)]
    if rows_b:
        low_b, tot_b, post_b = part(got_b)
        low_b = rotate_rows(low_b, SHIFTS)
        tot_a = tot_a + tot_b
        back.append(post_b.reshape(count_dom, rows_b, post_width))
    back = jnp.concatenate(back, axis=1)
    got_back = lax.all_to_all(back, "dom", 0, 0, tiled=True).reshape(count_dom * capacity, post_width)

    if not rows_b:
        low_b = jnp.zeros((SHIFTS * rows, 8), jnp.bfloat16)
        got_b = jnp.zeros((8, width), particles.dtype)
    tot_a = rotate_rows(tot_a, 1)
    tail = jnp.zeros((rows, IMG), jnp.bfloat16)
    for q, piece in enumerate(split_bf16(tot_a)):
        tail = tail.at[:, q].set(piece)
    outgoing = last_sums(low_b, got_b, sums_a, tail, offsets, pixels, count_ref)
    pieces = [outgoing[0]] + [ahead(outgoing[k], "ref", k) for k in range(1, count_ref)]
    class_sums = sum(piece[:, :pixels].reshape(projections.shape).astype(f32) for piece in pieces)
    class_sums = class_sums.astype(jnp.bfloat16)
    weight_totals = sum(
        piece[:, pixels].astype(f32) + piece[:, pixels + 1].astype(f32) + piece[:, pixels + 2].astype(f32)
        for piece in pieces
    ).reshape(projections.shape[0], projections.shape[1])

    mine = got_back[owners * capacity + slot_rank]
    class_prob = mine[:, : post_width - 1]
    log_like = mine[:, post_width - 1]
    return (class_prob, log_like, class_sums, weight_totals)


def solution(mesh):
    in_specs = (
        P(("dom", "ref"), None),
        P(("dom", "ref")),
        P(("dom", "ref")),
        P(("dom", "ref")),
        P("ref", "dom", None),
        P("dom"),
    )
    out_specs = (P(("dom", "ref"), None), P(("dom", "ref")), P("ref", "dom", None), P("ref", "dom"))
    return jax.shard_map(shards, mesh=mesh, in_specs=in_specs, out_specs=out_specs, check_vma=False)
```

```python
import functools

import jax
import jax.numpy as jnp
from jax import lax
from jax.experimental import pallas as pl
from jax.experimental.pallas import tpu as pltpu
from jax.sharding import PartitionSpec as P

IMG = 128
SHIFTS = 3
PRIOR_WIDTH = 576
FIRST_ROWS = 8
CHUNK = 2048


def translate(images, offset):
    if offset == 0:
        return images
    pixels = images.shape[-1]
    lane = lax.broadcasted_iota(jnp.int32, images.shape, images.ndim - 1) % IMG
    near = jnp.roll(images, offset, axis=-1)
    if offset > 0:
        far = jnp.roll(images, offset - IMG, axis=-1)
        keep = lane >= offset
    else:
        far = jnp.roll(images, offset + IMG, axis=-1)
        keep = lane < IMG + offset
    del pixels
    return jnp.where(keep, near, far)


def rolled_sum(y, rows, offsets, lanes):
    acc = None
    for u, t in enumerate(offsets):
        blk = y[u * rows:(u + 1) * rows, lanes * IMG:(lanes + 1) * IMG]
        if t % IMG:
            blk = pltpu.roll(blk, shift=t % IMG, axis=1)
        acc = blk if acc is None else acc + blk
    return acc


def first_sums_kernel(offsets, rows, w_ref, x_ref, out_ref):
    y = jnp.dot(w_ref[...], x_ref[...], preferred_element_type=jnp.float32)
    for j in range(out_ref.shape[1] // IMG):
        out_ref[:, j * IMG:(j + 1) * IMG] = rolled_sum(y, rows, offsets, j)


def last_sums_kernel(offsets, rows, chunk, w_ref, x_ref, acc_ref, tail_ref, *refs):
    out_refs, moved_ref = refs[:-1], refs[-1]
    k = pl.program_id(0)
    n = x_ref.shape[0]
    x = x_ref[...]
    wide = x.astype(jnp.float32)
    for u, t in enumerate(offsets):
        if t % IMG:
            for j in range(chunk // IMG):
                piece = pltpu.roll(wide[:, j * IMG:(j + 1) * IMG], shift=t % IMG, axis=1)
                moved_ref[u * n:(u + 1) * n, j * IMG:(j + 1) * IMG] = piece.astype(moved_ref.dtype)
        else:
            moved_ref[u * n:(u + 1) * n, :] = x
    total = acc_ref[...] + jnp.dot(w_ref[...], moved_ref[...], preferred_element_type=jnp.float32)
    group = rows // len(out_refs)
    for q, out_ref in enumerate(out_refs):
        pixels = out_ref.shape[1] - tail_ref.shape[1]
        out_ref[:, pl.ds(k * chunk, chunk)] = total[q * group:(q + 1) * group].astype(out_ref.dtype)
        out_ref[:, pixels:] = tail_ref[q * group:(q + 1) * group]


def first_sums(w, x, offsets, pixels):
    rows = w.shape[0] // len(offsets)
    chunk = min(CHUNK, pixels)
    return pl.pallas_call(
        functools.partial(first_sums_kernel, tuple(offsets), rows),
        grid=(pixels // chunk,),
        in_specs=[
            pl.BlockSpec(w.shape, lambda k: (0, 0)),
            pl.BlockSpec((x.shape[0], chunk), lambda k: (0, k)),
        ],
        out_specs=pl.BlockSpec((rows, chunk), lambda k: (0, k)),
        out_shape=jax.ShapeDtypeStruct((rows, pixels), jnp.float32),
        cost_estimate=pl.CostEstimate(
            flops=2 * w.shape[0] * pixels * x.shape[0],
            transcendentals=0,
            bytes_accessed=2 * (x.shape[0] * pixels + w.size) + 4 * rows * pixels,
        ),
    )(w, x)


def last_sums(w, x, acc, tail, offsets, pixels, blocks):
    rows = acc.shape[0]
    group = rows // blocks
    chunk = min(CHUNK, pixels)
    width = pixels + tail.shape[1]
    n = x.shape[0]
    stacked_w = w.reshape(len(offsets), rows, n).transpose(1, 0, 2).reshape(rows, len(offsets) * n)
    return pl.pallas_call(
        functools.partial(last_sums_kernel, tuple(offsets), rows, chunk),
        grid=(pixels // chunk,),
        in_specs=[
            pl.BlockSpec(stacked_w.shape, lambda k: (0, 0)),
            pl.BlockSpec((n, chunk), lambda k: (0, k)),
            pl.BlockSpec((rows, chunk), lambda k: (0, k)),
            pl.BlockSpec(tail.shape, lambda k: (0, 0)),
        ],
        out_specs=[pl.BlockSpec((group, width), lambda k: (0, 0)) for _ in range(blocks)],
        out_shape=[jax.ShapeDtypeStruct((group, width), jnp.bfloat16) for _ in range(blocks)],
        scratch_shapes=[pltpu.VMEM((len(offsets) * n, chunk), x.dtype)],
        cost_estimate=pl.CostEstimate(
            flops=2 * w.shape[0] * pixels * n,
            transcendentals=0,
            bytes_accessed=2 * (n * width + w.size + rows * width) + 4 * rows * pixels,
        ),
    )(stacked_w, x, acc, tail)


def split_bf16(values):
    hi = values.astype(jnp.bfloat16)
    rest = values - hi.astype(jnp.float32)
    mid = rest.astype(jnp.bfloat16)
    lo = (rest - mid.astype(jnp.float32)).astype(jnp.bfloat16)
    return [hi, mid, lo]


def ahead(block, axis, distance):
    size = lax.axis_size(axis)
    return lax.ppermute(block, axis, [(i, (i + distance) % size) for i in range(size)])


def shards(particles, noise_prec, prior_pose, owners, projections, pose_index):
    f32 = jnp.float32
    count_dom = lax.axis_size("dom")
    count_ref = lax.axis_size("ref")
    arrived, pixels = particles.shape
    capacity = (5 * arrived + 4 * count_dom - 1) // (4 * count_dom)
    rows_a = min(FIRST_ROWS, capacity)
    rows_b = capacity - rows_a

    earlier = jnp.arange(arrived)[:, None] > jnp.arange(arrived)[None, :]
    same_owner = owners[:, None] == owners[None, :]
    slot_rank = jnp.sum(same_owner & earlier, axis=1).astype(jnp.int32)
    in_a = slot_rank < rows_a

    def pick(slot_of, count):
        return slot_of[None, :] == jnp.arange(count, dtype=jnp.int32)[:, None]

    code = prior_pose + 1
    lane = jnp.arange(IMG, dtype=jnp.int32)[None, :]
    extra = jnp.where(lane == 0, noise_prec.astype(f32)[:, None], 0.0)
    extra = jnp.where(lane == 1, (code // 64).astype(f32)[:, None], extra)
    extra = jnp.where(lane == 2, (code % 64).astype(f32)[:, None], extra)
    carried = jnp.concatenate([particles, extra.astype(particles.dtype)], axis=1)
    width = pixels + IMG

    pick_a = pick(jnp.where(in_a, owners * rows_a + slot_rank, -1), count_dom * rows_a)
    send_a = jnp.dot(pick_a.astype(particles.dtype), carried, preferred_element_type=f32)
    send_a = send_a.astype(particles.dtype).reshape(count_dom, rows_a, width)
    got_a = lax.all_to_all(send_a, "dom", 0, 0, tiled=True).reshape(count_dom * rows_a, width)
    _, own_proj = lax.optimization_barrier((send_a, projections.reshape(-1, pixels)))
    ref_here = lax.axis_index("ref")
    blocks = jnp.zeros((count_ref,) + own_proj.shape, own_proj.dtype)
    blocks = lax.dynamic_update_index_in_dim(blocks, own_proj, ref_here, 0)
    for k in range(1, count_ref):
        moved = ahead(own_proj, "ref", k)
        blocks = lax.dynamic_update_index_in_dim(blocks, moved, (ref_here - k) % count_ref, 0)
    all_proj = blocks.reshape(-1, pixels)
    if rows_b:
        pick_b = pick(jnp.where(in_a, -1, owners * rows_b + slot_rank - rows_a), count_dom * rows_b)
        all_proj, pick_b = lax.optimization_barrier((all_proj, pick_b))
        send_b = jnp.dot(pick_b.astype(particles.dtype), carried, preferred_element_type=f32)
        send_b = send_b.astype(particles.dtype).reshape(count_dom, rows_b, width)
        got_a, send_b = lax.optimization_barrier((got_a, send_b))
        got_b = lax.all_to_all(send_b, "dom", 0, 0, tiled=True).reshape(count_dom * rows_b, width)

    rows = all_proj.shape[0]
    offsets = [u - SHIFTS // 2 for u in range(SHIFTS)]
    shifted = jnp.concatenate([translate(all_proj, -t) for t in offsets], axis=0)
    norms = jnp.sum(jnp.square(all_proj.astype(f32)), axis=1)
    per_class = projections.shape[1]
    pose_f = pose_index.astype(f32)

    def part(received):
        n = received.shape[0]
        precision = received[:, pixels].astype(f32)
        prior_ids = received[:, pixels + 1].astype(f32) * 64.0 + received[:, pixels + 2].astype(f32) - 1.0
        live = (prior_ids >= 0).astype(f32)
        corr = lax.dot_general(
            received[:, :pixels], shifted, (((1,), (1,)), ((), ())), preferred_element_type=f32
        ).reshape(n, SHIFTS, rows)
        log_prior = -jnp.abs(pose_f[None, :] - prior_ids[:, None]) / PRIOR_WIDTH
        prior_rows = jnp.tile(log_prior, (1, rows // per_class))
        scaled = corr / IMG - norms[None, None, :] / (2.0 * IMG * IMG)
        scores = precision[:, None, None] * scaled + prior_rows[:, None, :]
        highest = jnp.max(scores, axis=(1, 2))
        loglike = highest + jnp.log(jnp.sum(jnp.exp(scores - highest[:, None, None]), axis=(1, 2)))
        weights = jnp.exp(scores - loglike[:, None, None]) * live[:, None, None]
        class_post = jnp.sum(weights.reshape(n, SHIFTS, rows // per_class, per_class), axis=(1, 3))
        totals = jnp.sum(weights, axis=(0, 1))
        low = weights.astype(jnp.bfloat16).reshape(n, SHIFTS * rows).T
        post = jnp.concatenate([class_post, loglike[:, None]], axis=1)
        return low, totals, post

    order = (ref_here + jnp.arange(count_ref, dtype=jnp.int32)) % count_ref

    def rotate_rows(values, lead):
        shape = values.shape
        grouped = values.reshape((lead, count_ref, -1) + shape[1:])
        return jnp.take(grouped, order, axis=1).reshape(shape)

    low_a, tot_a, post_a = part(got_a)
    low_a = rotate_rows(low_a, SHIFTS)
    sums_a = first_sums(low_a, got_a, offsets, pixels)
    post_width = post_a.shape[1]
    back = [post_a.reshape(count_dom, rows_a, post_width)]
    if rows_b:
        low_b, tot_b, post_b = part(got_b)
        low_b = rotate_rows(low_b, SHIFTS)
        tot_a = tot_a + tot_b
        back.append(post_b.reshape(count_dom, rows_b, post_width))
    back = jnp.concatenate(back, axis=1)
    got_back = lax.all_to_all(back, "dom", 0, 0, tiled=True).reshape(count_dom * capacity, post_width)

    if not rows_b:
        low_b = jnp.zeros((SHIFTS * rows, 8), jnp.bfloat16)
        got_b = jnp.zeros((8, width), particles.dtype)
    tot_a = rotate_rows(tot_a, 1)
    tail = jnp.zeros((rows, IMG), jnp.bfloat16)
    for q, piece in enumerate(split_bf16(tot_a)):
        tail = tail.at[:, q].set(piece)
    outgoing = last_sums(low_b, got_b, sums_a, tail, offsets, pixels, count_ref)
    pieces = [outgoing[0]] + [ahead(outgoing[k], "ref", k) for k in range(1, count_ref)]
    class_sums = sum(piece[:, :pixels].reshape(projections.shape).astype(f32) for piece in pieces)
    class_sums = class_sums.astype(jnp.bfloat16)
    weight_totals = sum(
        piece[:, pixels].astype(f32) + piece[:, pixels + 1].astype(f32) + piece[:, pixels + 2].astype(f32)
        for piece in pieces
    ).reshape(projections.shape[0], projections.shape[1])

    mine = got_back[owners * capacity + slot_rank]
    class_prob = mine[:, : post_width - 1]
    log_like = mine[:, post_width - 1]
    return (class_prob, log_like, class_sums, weight_totals)


def solution(mesh):
    in_specs = (
        P(("dom", "ref"), None),
        P(("dom", "ref")),
        P(("dom", "ref")),
        P(("dom", "ref")),
        P("ref", "dom", None),
        P("dom"),
    )
    out_specs = (P(("dom", "ref"), None), P(("dom", "ref")), P("ref", "dom", None), P("ref", "dom"))
    return jax.shard_map(shards, mesh=mesh, in_specs=in_specs, out_specs=out_specs, check_vma=False)
```

```python
import functools

import jax
import jax.numpy as jnp
from jax import lax
from jax.experimental import pallas as pl
from jax.experimental.pallas import tpu as pltpu
from jax.sharding import PartitionSpec as P

IMG = 128
SHIFTS = 3
PRIOR_WIDTH = 576
FIRST_ROWS = 8
CHUNK = 2048


def translate(images, offset):
    if offset == 0:
        return images
    pixels = images.shape[-1]
    lane = lax.broadcasted_iota(jnp.int32, images.shape, images.ndim - 1) % IMG
    near = jnp.roll(images, offset, axis=-1)
    if offset > 0:
        far = jnp.roll(images, offset - IMG, axis=-1)
        keep = lane >= offset
    else:
        far = jnp.roll(images, offset + IMG, axis=-1)
        keep = lane < IMG + offset
    del pixels
    return jnp.where(keep, near, far)


def rolled_sum(y, rows, offsets, lanes):
    acc = None
    for u, t in enumerate(offsets):
        blk = y[u * rows:(u + 1) * rows, lanes * IMG:(lanes + 1) * IMG]
        if t % IMG:
            blk = pltpu.roll(blk, shift=t % IMG, axis=1)
        acc = blk if acc is None else acc + blk
    return acc


def first_sums_kernel(offsets, rows, w_ref, x_ref, out_ref):
    y = jnp.dot(w_ref[...], x_ref[...], preferred_element_type=jnp.float32)
    for j in range(out_ref.shape[1] // IMG):
        out_ref[:, j * IMG:(j + 1) * IMG] = rolled_sum(y, rows, offsets, j)


def last_sums_kernel(offsets, rows, chunk, w_ref, x_ref, acc_ref, tail_ref, *out_refs):
    k = pl.program_id(0)
    y = jnp.dot(w_ref[...], x_ref[...], preferred_element_type=jnp.float32)
    group = rows // len(out_refs)
    for j in range(chunk // IMG):
        total = acc_ref[:, j * IMG:(j + 1) * IMG] + rolled_sum(y, rows, offsets, j)
        for q, out_ref in enumerate(out_refs):
            out_ref[:, pl.ds(k * chunk + j * IMG, IMG)] = total[q * group:(q + 1) * group].astype(
                out_ref.dtype
            )
    for q, out_ref in enumerate(out_refs):
        pixels = out_ref.shape[1] - tail_ref.shape[1]
        out_ref[:, pixels:] = tail_ref[q * group:(q + 1) * group]


def first_sums(w, x, offsets, pixels):
    rows = w.shape[0] // len(offsets)
    chunk = min(CHUNK, pixels)
    return pl.pallas_call(
        functools.partial(first_sums_kernel, tuple(offsets), rows),
        grid=(pixels // chunk,),
        in_specs=[
            pl.BlockSpec(w.shape, lambda k: (0, 0)),
            pl.BlockSpec((x.shape[0], chunk), lambda k: (0, k)),
        ],
        out_specs=pl.BlockSpec((rows, chunk), lambda k: (0, k)),
        out_shape=jax.ShapeDtypeStruct((rows, pixels), jnp.float32),
        cost_estimate=pl.CostEstimate(
            flops=2 * w.shape[0] * pixels * x.shape[0],
            transcendentals=0,
            bytes_accessed=2 * (x.shape[0] * pixels + w.size) + 4 * rows * pixels,
        ),
    )(w, x)


def last_sums(w, x, acc, tail, offsets, pixels, blocks):
    rows = acc.shape[0]
    group = rows // blocks
    chunk = min(CHUNK, pixels)
    width = pixels + tail.shape[1]
    n = x.shape[0]
    return pl.pallas_call(
        functools.partial(last_sums_kernel, tuple(offsets), rows, chunk),
        grid=(pixels // chunk,),
        in_specs=[
            pl.BlockSpec(w.shape, lambda k: (0, 0)),
            pl.BlockSpec((n, chunk), lambda k: (0, k)),
            pl.BlockSpec((rows, chunk), lambda k: (0, k)),
            pl.BlockSpec(tail.shape, lambda k: (0, 0)),
        ],
        out_specs=[pl.BlockSpec((group, width), lambda k: (0, 0)) for _ in range(blocks)],
        out_shape=[jax.ShapeDtypeStruct((group, width), jnp.bfloat16) for _ in range(blocks)],
        cost_estimate=pl.CostEstimate(
            flops=2 * w.shape[0] * pixels * n,
            transcendentals=0,
            bytes_accessed=2 * (n * pixels + w.size + rows * width) + 4 * rows * pixels,
        ),
    )(w, x, acc, tail)


def split_bf16(values):
    hi = values.astype(jnp.bfloat16)
    rest = values - hi.astype(jnp.float32)
    mid = rest.astype(jnp.bfloat16)
    lo = (rest - mid.astype(jnp.float32)).astype(jnp.bfloat16)
    return [hi, mid, lo]


def ahead(block, axis, distance):
    size = lax.axis_size(axis)
    return lax.ppermute(block, axis, [(i, (i + distance) % size) for i in range(size)])


def shards(particles, noise_prec, prior_pose, owners, projections, pose_index):
    f32 = jnp.float32
    count_dom = lax.axis_size("dom")
    count_ref = lax.axis_size("ref")
    arrived, pixels = particles.shape
    capacity = (5 * arrived + 4 * count_dom - 1) // (4 * count_dom)
    rows_a = min(FIRST_ROWS, capacity - 1)
    rows_b = capacity - rows_a

    earlier = jnp.arange(arrived)[:, None] > jnp.arange(arrived)[None, :]
    same_owner = owners[:, None] == owners[None, :]
    slot_rank = jnp.sum(same_owner & earlier, axis=1).astype(jnp.int32)
    in_a = slot_rank < rows_a

    def pick(slot_of, count):
        return slot_of[None, :] == jnp.arange(count, dtype=jnp.int32)[:, None]

    code = prior_pose + 1
    lane = jnp.arange(IMG, dtype=jnp.int32)[None, :]
    extra = jnp.where(lane == 0, noise_prec.astype(f32)[:, None], 0.0)
    extra = jnp.where(lane == 1, (code // 64).astype(f32)[:, None], extra)
    extra = jnp.where(lane == 2, (code % 64).astype(f32)[:, None], extra)
    carried = jnp.concatenate([particles, extra.astype(particles.dtype)], axis=1)
    width = pixels + IMG

    pick_b = pick(jnp.where(in_a, -1, owners * rows_b + slot_rank - rows_a), count_dom * rows_b)
    send_b = jnp.dot(pick_b.astype(particles.dtype), carried, preferred_element_type=f32)
    send_b = send_b.astype(particles.dtype).reshape(count_dom, rows_b, width)
    got_b = lax.all_to_all(send_b, "dom", 0, 0, tiled=True).reshape(count_dom * rows_b, width)
    _, own_proj = lax.optimization_barrier((send_b, projections.reshape(-1, pixels)))
    ref_here = lax.axis_index("ref")
    blocks = jnp.zeros((count_ref,) + own_proj.shape, own_proj.dtype)
    blocks = lax.dynamic_update_index_in_dim(blocks, own_proj, ref_here, 0)
    for k in range(1, count_ref):
        moved = ahead(own_proj, "ref", k)
        blocks = lax.dynamic_update_index_in_dim(blocks, moved, (ref_here - k) % count_ref, 0)
    all_proj = blocks.reshape(-1, pixels)
    pick_a = pick(jnp.where(in_a, owners * rows_a + slot_rank, -1), count_dom * rows_a)
    all_proj, pick_a = lax.optimization_barrier((all_proj, pick_a))
    send_a = jnp.dot(pick_a.astype(particles.dtype), carried, preferred_element_type=f32)
    send_a = send_a.astype(particles.dtype).reshape(count_dom, rows_a, width)
    got_b, send_a = lax.optimization_barrier((got_b, send_a))
    got_a = lax.all_to_all(send_a, "dom", 0, 0, tiled=True).reshape(count_dom * rows_a, width)

    rows = all_proj.shape[0]
    offsets = [u - SHIFTS // 2 for u in range(SHIFTS)]
    shifted = jnp.concatenate([translate(all_proj, -t) for t in offsets], axis=0)
    norms = jnp.sum(jnp.square(all_proj.astype(f32)), axis=1)
    per_class = projections.shape[1]
    pose_f = pose_index.astype(f32)

    def part(received):
        n = received.shape[0]
        precision = received[:, pixels].astype(f32)
        prior_ids = received[:, pixels + 1].astype(f32) * 64.0 + received[:, pixels + 2].astype(f32) - 1.0
        live = (prior_ids >= 0).astype(f32)
        corr = lax.dot_general(
            received[:, :pixels], shifted, (((1,), (1,)), ((), ())), preferred_element_type=f32
        ).reshape(n, SHIFTS, rows)
        log_prior = -jnp.abs(pose_f[None, :] - prior_ids[:, None]) / PRIOR_WIDTH
        prior_rows = jnp.tile(log_prior, (1, rows // per_class))
        scaled = corr / IMG - norms[None, None, :] / (2.0 * IMG * IMG)
        scores = precision[:, None, None] * scaled + prior_rows[:, None, :]
        highest = jnp.max(scores, axis=(1, 2))
        loglike = highest + jnp.log(jnp.sum(jnp.exp(scores - highest[:, None, None]), axis=(1, 2)))
        weights = jnp.exp(scores - loglike[:, None, None]) * live[:, None, None]
        class_post = jnp.sum(weights.reshape(n, SHIFTS, rows // per_class, per_class), axis=(1, 3))
        totals = jnp.sum(weights, axis=(0, 1))
        low = weights.astype(jnp.bfloat16).reshape(n, SHIFTS * rows).T
        post = jnp.concatenate([class_post, loglike[:, None]], axis=1)
        return low, totals, post

    order = (ref_here + jnp.arange(count_ref, dtype=jnp.int32)) % count_ref

    def rotate_rows(values, lead):
        shape = values.shape
        grouped = values.reshape((lead, count_ref, -1) + shape[1:])
        return jnp.take(grouped, order, axis=1).reshape(shape)

    low_b, tot_b, post_b = part(got_b)
    sums_b = first_sums(rotate_rows(low_b, SHIFTS), got_b, offsets, pixels)
    low_a, tot_a, post_a = part(got_a)
    low_a = rotate_rows(low_a, SHIFTS)
    post_width = post_a.shape[1]
    back = jnp.concatenate(
        [post_a.reshape(count_dom, rows_a, post_width), post_b.reshape(count_dom, rows_b, post_width)],
        axis=1,
    )
    got_back = lax.all_to_all(back, "dom", 0, 0, tiled=True).reshape(count_dom * capacity, post_width)

    totals = rotate_rows(tot_a + tot_b, 1)
    tail = jnp.zeros((rows, IMG), jnp.bfloat16)
    for q, piece in enumerate(split_bf16(totals)):
        tail = tail.at[:, q].set(piece)
    outgoing = last_sums(low_a, got_a, sums_b, tail, offsets, pixels, count_ref)
    pieces = [outgoing[0]] + [ahead(outgoing[k], "ref", k) for k in range(1, count_ref)]
    class_sums = sum(piece[:, :pixels].reshape(projections.shape).astype(f32) for piece in pieces)
    class_sums = class_sums.astype(jnp.bfloat16)
    weight_totals = sum(
        piece[:, pixels].astype(f32) + piece[:, pixels + 1].astype(f32) + piece[:, pixels + 2].astype(f32)
        for piece in pieces
    ).reshape(projections.shape[0], projections.shape[1])

    mine = got_back[owners * capacity + slot_rank]
    class_prob = mine[:, : post_width - 1]
    log_like = mine[:, post_width - 1]
    return (class_prob, log_like, class_sums, weight_totals)


def solution(mesh):
    in_specs = (
        P(("dom", "ref"), None),
        P(("dom", "ref")),
        P(("dom", "ref")),
        P(("dom", "ref")),
        P("ref", "dom", None),
        P("dom"),
    )
    out_specs = (P(("dom", "ref"), None), P(("dom", "ref")), P("ref", "dom", None), P("ref", "dom"))
    return jax.shard_map(shards, mesh=mesh, in_specs=in_specs, out_specs=out_specs, check_vma=False)
```

```python
import functools

import jax
import jax.numpy as jnp
from jax import lax
from jax.experimental import pallas as pl
from jax.experimental.pallas import tpu as pltpu
from jax.sharding import PartitionSpec as P

IMG = 128
SHIFTS = 3
PRIOR_WIDTH = 576
FIRST_ROWS = 8
CHUNK = 4096


def translate(images, offset):
    if offset == 0:
        return images
    pixels = images.shape[-1]
    lane = lax.broadcasted_iota(jnp.int32, images.shape, images.ndim - 1) % IMG
    near = jnp.roll(images, offset, axis=-1)
    if offset > 0:
        far = jnp.roll(images, offset - IMG, axis=-1)
        keep = lane >= offset
    else:
        far = jnp.roll(images, offset + IMG, axis=-1)
        keep = lane < IMG + offset
    del pixels
    return jnp.where(keep, near, far)


def rolled_sum(y, rows, offsets, lanes):
    acc = None
    for u, t in enumerate(offsets):
        blk = y[u * rows:(u + 1) * rows, lanes * IMG:(lanes + 1) * IMG]
        if t % IMG:
            blk = pltpu.roll(blk, shift=t % IMG, axis=1)
        acc = blk if acc is None else acc + blk
    return acc


def first_sums_kernel(offsets, rows, w_ref, x_ref, out_ref):
    y = jnp.dot(w_ref[...], x_ref[...], preferred_element_type=jnp.float32)
    for j in range(out_ref.shape[1] // IMG):
        out_ref[:, j * IMG:(j + 1) * IMG] = rolled_sum(y, rows, offsets, j)


def last_sums_kernel(offsets, rows, chunk, w_ref, x_ref, acc_ref, tail_ref, *refs):
    out_refs, moved_ref = refs[:-1], refs[-1]
    k = pl.program_id(0)
    n = x_ref.shape[0]
    x = x_ref[...]
    wide = x.astype(jnp.float32)
    for u, t in enumerate(offsets):
        if t % IMG:
            for j in range(chunk // IMG):
                piece = pltpu.roll(wide[:, j * IMG:(j + 1) * IMG], shift=t % IMG, axis=1)
                moved_ref[u * n:(u + 1) * n, j * IMG:(j + 1) * IMG] = piece.astype(moved_ref.dtype)
        else:
            moved_ref[u * n:(u + 1) * n, :] = x
    total = acc_ref[...] + jnp.dot(w_ref[...], moved_ref[...], preferred_element_type=jnp.float32)
    group = rows // len(out_refs)
    for q, out_ref in enumerate(out_refs):
        pixels = out_ref.shape[1] - tail_ref.shape[1]
        out_ref[:, pl.ds(k * chunk, chunk)] = total[q * group:(q + 1) * group].astype(out_ref.dtype)
        out_ref[:, pixels:] = tail_ref[q * group:(q + 1) * group]


def first_sums(w, x, offsets, pixels):
    rows = w.shape[0] // len(offsets)
    chunk = min(CHUNK, pixels)
    return pl.pallas_call(
        functools.partial(first_sums_kernel, tuple(offsets), rows),
        grid=(pixels // chunk,),
        in_specs=[
            pl.BlockSpec(w.shape, lambda k: (0, 0)),
            pl.BlockSpec((x.shape[0], chunk), lambda k: (0, k)),
        ],
        out_specs=pl.BlockSpec((rows, chunk), lambda k: (0, k)),
        out_shape=jax.ShapeDtypeStruct((rows, pixels), jnp.float32),
        cost_estimate=pl.CostEstimate(
            flops=2 * w.shape[0] * pixels * x.shape[0],
            transcendentals=0,
            bytes_accessed=2 * (x.shape[0] * pixels + w.size) + 4 * rows * pixels,
        ),
    )(w, x)


def last_sums(w, x, acc, tail, offsets, pixels, blocks):
    rows = acc.shape[0]
    group = rows // blocks
    chunk = min(CHUNK, pixels)
    width = pixels + tail.shape[1]
    n = x.shape[0]
    stacked_w = w.reshape(len(offsets), rows, n).transpose(1, 0, 2).reshape(rows, len(offsets) * n)
    return pl.pallas_call(
        functools.partial(last_sums_kernel, tuple(offsets), rows, chunk),
        grid=(pixels // chunk,),
        in_specs=[
            pl.BlockSpec(stacked_w.shape, lambda k: (0, 0)),
            pl.BlockSpec((n, chunk), lambda k: (0, k)),
            pl.BlockSpec((rows, chunk), lambda k: (0, k)),
            pl.BlockSpec(tail.shape, lambda k: (0, 0)),
        ],
        out_specs=[pl.BlockSpec((group, width), lambda k: (0, 0)) for _ in range(blocks)],
        out_shape=[jax.ShapeDtypeStruct((group, width), jnp.bfloat16) for _ in range(blocks)],
        scratch_shapes=[pltpu.VMEM((len(offsets) * n, chunk), x.dtype)],
        cost_estimate=pl.CostEstimate(
            flops=2 * w.shape[0] * pixels * n,
            transcendentals=0,
            bytes_accessed=2 * (n * width + w.size + rows * width) + 4 * rows * pixels,
        ),
    )(stacked_w, x, acc, tail)


def split_bf16(values):
    hi = values.astype(jnp.bfloat16)
    rest = values - hi.astype(jnp.float32)
    mid = rest.astype(jnp.bfloat16)
    lo = (rest - mid.astype(jnp.float32)).astype(jnp.bfloat16)
    return [hi, mid, lo]


def ahead(block, axis, distance):
    size = lax.axis_size(axis)
    return lax.ppermute(block, axis, [(i, (i + distance) % size) for i in range(size)])


def shards(particles, noise_prec, prior_pose, owners, projections, pose_index):
    f32 = jnp.float32
    count_dom = lax.axis_size("dom")
    count_ref = lax.axis_size("ref")
    arrived, pixels = particles.shape
    capacity = (5 * arrived + 4 * count_dom - 1) // (4 * count_dom)
    rows_a = min(FIRST_ROWS, capacity)
    rows_b = capacity - rows_a

    earlier = jnp.arange(arrived)[:, None] > jnp.arange(arrived)[None, :]
    same_owner = owners[:, None] == owners[None, :]
    slot_rank = jnp.sum(same_owner & earlier, axis=1).astype(jnp.int32)
    in_a = slot_rank < rows_a

    def pick(slot_of, count):
        return slot_of[None, :] == jnp.arange(count, dtype=jnp.int32)[:, None]

    code = prior_pose + 1
    lane = jnp.arange(IMG, dtype=jnp.int32)[None, :]
    extra = jnp.where(lane == 0, noise_prec.astype(f32)[:, None], 0.0)
    extra = jnp.where(lane == 1, (code // 64).astype(f32)[:, None], extra)
    extra = jnp.where(lane == 2, (code % 64).astype(f32)[:, None], extra)
    carried = jnp.concatenate([particles, extra.astype(particles.dtype)], axis=1)
    width = pixels + IMG

    pick_a = pick(jnp.where(in_a, owners * rows_a + slot_rank, -1), count_dom * rows_a)
    send_a = jnp.dot(pick_a.astype(particles.dtype), carried, preferred_element_type=f32)
    send_a = send_a.astype(particles.dtype).reshape(count_dom, rows_a, width)
    got_a = lax.all_to_all(send_a, "dom", 0, 0, tiled=True).reshape(count_dom * rows_a, width)
    _, own_proj = lax.optimization_barrier((send_a, projections.reshape(-1, pixels)))
    ref_here = lax.axis_index("ref")
    blocks = jnp.zeros((count_ref,) + own_proj.shape, own_proj.dtype)
    blocks = lax.dynamic_update_index_in_dim(blocks, own_proj, ref_here, 0)
    for k in range(1, count_ref):
        moved = ahead(own_proj, "ref", k)
        blocks = lax.dynamic_update_index_in_dim(blocks, moved, (ref_here - k) % count_ref, 0)
    all_proj = blocks.reshape(-1, pixels)
    if rows_b:
        pick_b = pick(jnp.where(in_a, -1, owners * rows_b + slot_rank - rows_a), count_dom * rows_b)
        all_proj, pick_b = lax.optimization_barrier((all_proj, pick_b))
        send_b = jnp.dot(pick_b.astype(particles.dtype), carried, preferred_element_type=f32)
        send_b = send_b.astype(particles.dtype).reshape(count_dom, rows_b, width)
        got_a, send_b = lax.optimization_barrier((got_a, send_b))
        got_b = lax.all_to_all(send_b, "dom", 0, 0, tiled=True).reshape(count_dom * rows_b, width)

    rows = all_proj.shape[0]
    offsets = [u - SHIFTS // 2 for u in range(SHIFTS)]
    shifted = jnp.concatenate([translate(all_proj, -t) for t in offsets], axis=0)
    norms = jnp.sum(jnp.square(all_proj.astype(f32)), axis=1)
    per_class = projections.shape[1]
    pose_f = pose_index.astype(f32)

    def part(received):
        n = received.shape[0]
        precision = received[:, pixels].astype(f32)
        prior_ids = received[:, pixels + 1].astype(f32) * 64.0 + received[:, pixels + 2].astype(f32) - 1.0
        live = (prior_ids >= 0).astype(f32)
        corr = lax.dot_general(
            received[:, :pixels], shifted, (((1,), (1,)), ((), ())), preferred_element_type=f32
        ).reshape(n, SHIFTS, rows)
        log_prior = -jnp.abs(pose_f[None, :] - prior_ids[:, None]) / PRIOR_WIDTH
        prior_rows = jnp.tile(log_prior, (1, rows // per_class))
        scaled = corr / IMG - norms[None, None, :] / (2.0 * IMG * IMG)
        scores = precision[:, None, None] * scaled + prior_rows[:, None, :]
        highest = jnp.max(scores, axis=(1, 2))
        loglike = highest + jnp.log(jnp.sum(jnp.exp(scores - highest[:, None, None]), axis=(1, 2)))
        weights = jnp.exp(scores - loglike[:, None, None]) * live[:, None, None]
        class_post = jnp.sum(weights.reshape(n, SHIFTS, rows // per_class, per_class), axis=(1, 3))
        totals = jnp.sum(weights, axis=(0, 1))
        low = weights.astype(jnp.bfloat16).reshape(n, SHIFTS * rows).T
        post = jnp.concatenate([class_post, loglike[:, None]], axis=1)
        return low, totals, post

    order = (ref_here + jnp.arange(count_ref, dtype=jnp.int32)) % count_ref

    def rotate_rows(values, lead):
        shape = values.shape
        grouped = values.reshape((lead, count_ref, -1) + shape[1:])
        return jnp.take(grouped, order, axis=1).reshape(shape)

    low_a, tot_a, post_a = part(got_a)
    low_a = rotate_rows(low_a, SHIFTS)
    sums_a = first_sums(low_a, got_a, offsets, pixels)
    post_width = post_a.shape[1]
    back = [post_a.reshape(count_dom, rows_a, post_width)]
    if rows_b:
        low_b, tot_b, post_b = part(got_b)
        low_b = rotate_rows(low_b, SHIFTS)
        tot_a = tot_a + tot_b
        back.append(post_b.reshape(count_dom, rows_b, post_width))
    back = jnp.concatenate(back, axis=1)
    got_back = lax.all_to_all(back, "dom", 0, 0, tiled=True).reshape(count_dom * capacity, post_width)

    if not rows_b:
        low_b = jnp.zeros((SHIFTS * rows, 8), jnp.bfloat16)
        got_b = jnp.zeros((8, width), particles.dtype)
    tot_a = rotate_rows(tot_a, 1)
    tail = jnp.zeros((rows, IMG), jnp.bfloat16)
    for q, piece in enumerate(split_bf16(tot_a)):
        tail = tail.at[:, q].set(piece)
    outgoing = last_sums(low_b, got_b, sums_a, tail, offsets, pixels, count_ref)
    pieces = [outgoing[0]] + [ahead(outgoing[k], "ref", k) for k in range(1, count_ref)]
    class_sums = sum(piece[:, :pixels].reshape(projections.shape).astype(f32) for piece in pieces)
    class_sums = class_sums.astype(jnp.bfloat16)
    weight_totals = sum(
        piece[:, pixels].astype(f32) + piece[:, pixels + 1].astype(f32) + piece[:, pixels + 2].astype(f32)
        for piece in pieces
    ).reshape(projections.shape[0], projections.shape[1])

    mine = got_back[owners * capacity + slot_rank]
    class_prob = mine[:, : post_width - 1]
    log_like = mine[:, post_width - 1]
    return (class_prob, log_like, class_sums, weight_totals)


def solution(mesh):
    in_specs = (
        P(("dom", "ref"), None),
        P(("dom", "ref")),
        P(("dom", "ref")),
        P(("dom", "ref")),
        P("ref", "dom", None),
        P("dom"),
    )
    out_specs = (P(("dom", "ref"), None), P(("dom", "ref")), P("ref", "dom", None), P("ref", "dom"))
    return jax.shard_map(shards, mesh=mesh, in_specs=in_specs, out_specs=out_specs, check_vma=False)
```

```python
import functools

import jax
import jax.numpy as jnp
from jax import lax
from jax.experimental import pallas as pl
from jax.experimental.pallas import tpu as pltpu
from jax.sharding import PartitionSpec as P

IMG = 128
SHIFTS = 3
PRIOR_WIDTH = 576
FIRST_ROWS = 8
CHUNK = 8192


def translate(images, offset):
    if offset == 0:
        return images
    pixels = images.shape[-1]
    lane = lax.broadcasted_iota(jnp.int32, images.shape, images.ndim - 1) % IMG
    near = jnp.roll(images, offset, axis=-1)
    if offset > 0:
        far = jnp.roll(images, offset - IMG, axis=-1)
        keep = lane >= offset
    else:
        far = jnp.roll(images, offset + IMG, axis=-1)
        keep = lane < IMG + offset
    del pixels
    return jnp.where(keep, near, far)


def rolled_sum(y, rows, offsets, lanes):
    acc = None
    for u, t in enumerate(offsets):
        blk = y[u * rows:(u + 1) * rows, lanes * IMG:(lanes + 1) * IMG]
        if t % IMG:
            blk = pltpu.roll(blk, shift=t % IMG, axis=1)
        acc = blk if acc is None else acc + blk
    return acc


def first_sums_kernel(offsets, rows, w_ref, x_ref, out_ref):
    y = jnp.dot(w_ref[...], x_ref[...], preferred_element_type=jnp.float32)
    for j in range(out_ref.shape[1] // IMG):
        out_ref[:, j * IMG:(j + 1) * IMG] = rolled_sum(y, rows, offsets, j)


def last_sums_kernel(offsets, rows, chunk, w_ref, x_ref, acc_ref, tail_ref, *refs):
    out_refs, moved_ref = refs[:-1], refs[-1]
    k = pl.program_id(0)
    n = x_ref.shape[0]
    x = x_ref[...]
    wide = x.astype(jnp.float32)
    for u, t in enumerate(offsets):
        if t % IMG:
            for j in range(chunk // IMG):
                piece = pltpu.roll(wide[:, j * IMG:(j + 1) * IMG], shift=t % IMG, axis=1)
                moved_ref[u * n:(u + 1) * n, j * IMG:(j + 1) * IMG] = piece.astype(moved_ref.dtype)
        else:
            moved_ref[u * n:(u + 1) * n, :] = x
    total = acc_ref[...] + jnp.dot(w_ref[...], moved_ref[...], preferred_element_type=jnp.float32)
    group = rows // len(out_refs)
    for q, out_ref in enumerate(out_refs):
        pixels = out_ref.shape[1] - tail_ref.shape[1]
        out_ref[:, pl.ds(k * chunk, chunk)] = total[q * group:(q + 1) * group].astype(out_ref.dtype)
        out_ref[:, pixels:] = tail_ref[q * group:(q + 1) * group]


def first_sums(w, x, offsets, pixels):
    rows = w.shape[0] // len(offsets)
    chunk = min(CHUNK, pixels)
    return pl.pallas_call(
        functools.partial(first_sums_kernel, tuple(offsets), rows),
        grid=(pixels // chunk,),
        in_specs=[
            pl.BlockSpec(w.shape, lambda k: (0, 0)),
            pl.BlockSpec((x.shape[0], chunk), lambda k: (0, k)),
        ],
        out_specs=pl.BlockSpec((rows, chunk), lambda k: (0, k)),
        out_shape=jax.ShapeDtypeStruct((rows, pixels), jnp.float32),
        cost_estimate=pl.CostEstimate(
            flops=2 * w.shape[0] * pixels * x.shape[0],
            transcendentals=0,
            bytes_accessed=2 * (x.shape[0] * pixels + w.size) + 4 * rows * pixels,
        ),
    )(w, x)


def last_sums(w, x, acc, tail, offsets, pixels, blocks):
    rows = acc.shape[0]
    group = rows // blocks
    chunk = min(CHUNK, pixels)
    width = pixels + tail.shape[1]
    n = x.shape[0]
    stacked_w = w.reshape(len(offsets), rows, n).transpose(1, 0, 2).reshape(rows, len(offsets) * n)
    return pl.pallas_call(
        functools.partial(last_sums_kernel, tuple(offsets), rows, chunk),
        grid=(pixels // chunk,),
        in_specs=[
            pl.BlockSpec(stacked_w.shape, lambda k: (0, 0)),
            pl.BlockSpec((n, chunk), lambda k: (0, k)),
            pl.BlockSpec((rows, chunk), lambda k: (0, k)),
            pl.BlockSpec(tail.shape, lambda k: (0, 0)),
        ],
        out_specs=[pl.BlockSpec((group, width), lambda k: (0, 0)) for _ in range(blocks)],
        out_shape=[jax.ShapeDtypeStruct((group, width), jnp.bfloat16) for _ in range(blocks)],
        scratch_shapes=[pltpu.VMEM((len(offsets) * n, chunk), x.dtype)],
        cost_estimate=pl.CostEstimate(
            flops=2 * w.shape[0] * pixels * n,
            transcendentals=0,
            bytes_accessed=2 * (n * width + w.size + rows * width) + 4 * rows * pixels,
        ),
    )(stacked_w, x, acc, tail)


def split_bf16(values):
    hi = values.astype(jnp.bfloat16)
    rest = values - hi.astype(jnp.float32)
    mid = rest.astype(jnp.bfloat16)
    lo = (rest - mid.astype(jnp.float32)).astype(jnp.bfloat16)
    return [hi, mid, lo]


def ahead(block, axis, distance):
    size = lax.axis_size(axis)
    return lax.ppermute(block, axis, [(i, (i + distance) % size) for i in range(size)])


def shards(particles, noise_prec, prior_pose, owners, projections, pose_index):
    f32 = jnp.float32
    count_dom = lax.axis_size("dom")
    count_ref = lax.axis_size("ref")
    arrived, pixels = particles.shape
    capacity = (5 * arrived + 4 * count_dom - 1) // (4 * count_dom)
    rows_a = min(FIRST_ROWS, capacity)
    rows_b = capacity - rows_a

    earlier = jnp.arange(arrived)[:, None] > jnp.arange(arrived)[None, :]
    same_owner = owners[:, None] == owners[None, :]
    slot_rank = jnp.sum(same_owner & earlier, axis=1).astype(jnp.int32)
    in_a = slot_rank < rows_a

    def pick(slot_of, count):
        return slot_of[None, :] == jnp.arange(count, dtype=jnp.int32)[:, None]

    code = prior_pose + 1
    lane = jnp.arange(IMG, dtype=jnp.int32)[None, :]
    extra = jnp.where(lane == 0, noise_prec.astype(f32)[:, None], 0.0)
    extra = jnp.where(lane == 1, (code // 64).astype(f32)[:, None], extra)
    extra = jnp.where(lane == 2, (code % 64).astype(f32)[:, None], extra)
    carried = jnp.concatenate([particles, extra.astype(particles.dtype)], axis=1)
    width = pixels + IMG

    pick_a = pick(jnp.where(in_a, owners * rows_a + slot_rank, -1), count_dom * rows_a)
    send_a = jnp.dot(pick_a.astype(particles.dtype), carried, preferred_element_type=f32)
    send_a = send_a.astype(particles.dtype).reshape(count_dom, rows_a, width)
    got_a = lax.all_to_all(send_a, "dom", 0, 0, tiled=True).reshape(count_dom * rows_a, width)
    _, own_proj = lax.optimization_barrier((send_a, projections.reshape(-1, pixels)))
    ref_here = lax.axis_index("ref")
    blocks = jnp.zeros((count_ref,) + own_proj.shape, own_proj.dtype)
    blocks = lax.dynamic_update_index_in_dim(blocks, own_proj, ref_here, 0)
    for k in range(1, count_ref):
        moved = ahead(own_proj, "ref", k)
        blocks = lax.dynamic_update_index_in_dim(blocks, moved, (ref_here - k) % count_ref, 0)
    all_proj = blocks.reshape(-1, pixels)
    if rows_b:
        pick_b = pick(jnp.where(in_a, -1, owners * rows_b + slot_rank - rows_a), count_dom * rows_b)
        all_proj, pick_b = lax.optimization_barrier((all_proj, pick_b))
        send_b = jnp.dot(pick_b.astype(particles.dtype), carried, preferred_element_type=f32)
        send_b = send_b.astype(particles.dtype).reshape(count_dom, rows_b, width)
        got_a, send_b = lax.optimization_barrier((got_a, send_b))
        got_b = lax.all_to_all(send_b, "dom", 0, 0, tiled=True).reshape(count_dom * rows_b, width)

    rows = all_proj.shape[0]
    offsets = [u - SHIFTS // 2 for u in range(SHIFTS)]
    shifted = jnp.concatenate([translate(all_proj, -t) for t in offsets], axis=0)
    norms = jnp.sum(jnp.square(all_proj.astype(f32)), axis=1)
    per_class = projections.shape[1]
    pose_f = pose_index.astype(f32)

    def part(received):
        n = received.shape[0]
        precision = received[:, pixels].astype(f32)
        prior_ids = received[:, pixels + 1].astype(f32) * 64.0 + received[:, pixels + 2].astype(f32) - 1.0
        live = (prior_ids >= 0).astype(f32)
        corr = lax.dot_general(
            received[:, :pixels], shifted, (((1,), (1,)), ((), ())), preferred_element_type=f32
        ).reshape(n, SHIFTS, rows)
        log_prior = -jnp.abs(pose_f[None, :] - prior_ids[:, None]) / PRIOR_WIDTH
        prior_rows = jnp.tile(log_prior, (1, rows // per_class))
        scaled = corr / IMG - norms[None, None, :] / (2.0 * IMG * IMG)
        scores = precision[:, None, None] * scaled + prior_rows[:, None, :]
        highest = jnp.max(scores, axis=(1, 2))
        loglike = highest + jnp.log(jnp.sum(jnp.exp(scores - highest[:, None, None]), axis=(1, 2)))
        weights = jnp.exp(scores - loglike[:, None, None]) * live[:, None, None]
        class_post = jnp.sum(weights.reshape(n, SHIFTS, rows // per_class, per_class), axis=(1, 3))
        totals = jnp.sum(weights, axis=(0, 1))
        low = weights.astype(jnp.bfloat16).reshape(n, SHIFTS * rows).T
        post = jnp.concatenate([class_post, loglike[:, None]], axis=1)
        return low, totals, post

    order = (ref_here + jnp.arange(count_ref, dtype=jnp.int32)) % count_ref

    def rotate_rows(values, lead):
        shape = values.shape
        grouped = values.reshape((lead, count_ref, -1) + shape[1:])
        return jnp.take(grouped, order, axis=1).reshape(shape)

    low_a, tot_a, post_a = part(got_a)
    low_a = rotate_rows(low_a, SHIFTS)
    sums_a = first_sums(low_a, got_a, offsets, pixels)
    post_width = post_a.shape[1]
    back = [post_a.reshape(count_dom, rows_a, post_width)]
    if rows_b:
        low_b, tot_b, post_b = part(got_b)
        low_b = rotate_rows(low_b, SHIFTS)
        tot_a = tot_a + tot_b
        back.append(post_b.reshape(count_dom, rows_b, post_width))
    back = jnp.concatenate(back, axis=1)
    got_back = lax.all_to_all(back, "dom", 0, 0, tiled=True).reshape(count_dom * capacity, post_width)

    if not rows_b:
        low_b = jnp.zeros((SHIFTS * rows, 8), jnp.bfloat16)
        got_b = jnp.zeros((8, width), particles.dtype)
    tot_a = rotate_rows(tot_a, 1)
    tail = jnp.zeros((rows, IMG), jnp.bfloat16)
    for q, piece in enumerate(split_bf16(tot_a)):
        tail = tail.at[:, q].set(piece)
    outgoing = last_sums(low_b, got_b, sums_a, tail, offsets, pixels, count_ref)
    pieces = [outgoing[0]] + [ahead(outgoing[k], "ref", k) for k in range(1, count_ref)]
    class_sums = sum(piece[:, :pixels].reshape(projections.shape).astype(f32) for piece in pieces)
    class_sums = class_sums.astype(jnp.bfloat16)
    weight_totals = sum(
        piece[:, pixels].astype(f32) + piece[:, pixels + 1].astype(f32) + piece[:, pixels + 2].astype(f32)
        for piece in pieces
    ).reshape(projections.shape[0], projections.shape[1])

    mine = got_back[owners * capacity + slot_rank]
    class_prob = mine[:, : post_width - 1]
    log_like = mine[:, post_width - 1]
    return (class_prob, log_like, class_sums, weight_totals)


def solution(mesh):
    in_specs = (
        P(("dom", "ref"), None),
        P(("dom", "ref")),
        P(("dom", "ref")),
        P(("dom", "ref")),
        P("ref", "dom", None),
        P("dom"),
    )
    out_specs = (P(("dom", "ref"), None), P(("dom", "ref")), P("ref", "dom", None), P("ref", "dom"))
    return jax.shard_map(shards, mesh=mesh, in_specs=in_specs, out_specs=out_specs, check_vma=False)
```
